32 devices in a mesh: row: 4 (over z), col: 4 (over y, core), pix: 2 (over x).
Axes of the slice: x: 2, y: 2, z: 4, core: 2. Of those that a mesh axis runs over, the one named last changes fastest.
Arguments:
- sample_frames: bfloat16 [4096, 16384], P(('row', 'col'), 'pix'), may hold values from 0.14 to 26
- reference_frames: bfloat16 [4096, 16384], P(('row', 'col'), 'pix'), may hold values from 0.14 to 26
- gain: float32 [16384], P('pix'), may hold values from 0.5 to 2
- flat: float32 [16384], P('pix'), may hold values from 0.6 to 1.6
- qbin: int32 [16384], P('pix'), may hold values from 0 to 31
- region: int32 [16384], P('pix'), may hold values 0 or 1
- live: int32 [16384], P('pix'), may hold values 0 or 1
Outputs:
- twotime: float32 [4096, 4, 4, 256], P('row', None, 'col', 'pix')
The draws below stay inside these ranges and needn't reach their ends.
All inputs are finite; a program needn't handle non-finite values. No bound on the sum of `region` or of `live` on one device may be relied on, other than what follows from the above.
Results may differ from the reference program's by a relative error of at most 0.0039.
Values may be sent and summed in bfloat16 or wider, within the bound.
No kernel may reach another device: no remote copies, remote signals or barrier semaphores. Data moves between devices by JAX's collectives and lax.ppermute only.
A program may use at most 128 MiB of HBM per device.

```python
import math
import jax
import jax.numpy as jnp
from jax import lax

FRAMES = 4096
QBINS = 32
PIX = 16384
FINE = 256
N_ROW = 4
N_COL = 4


def pixel_gain(key):
    sub = jax.random.fold_in(key, 11)
    return jax.random.uniform(sub, (PIX,), jnp.float32, 0.6, 1.4)


def pixel_flat(key):
    sub = jax.random.fold_in(key, 23)
    return jnp.exp(jax.random.uniform(sub, (PIX,), jnp.float32, math.log(0.6), math.log(1.6)))


def raw_frames(key, stream):
    sub = jax.random.fold_in(key, stream)
    intensity = jnp.exp(jax.random.uniform(sub, (FRAMES, PIX), jnp.float32, math.log(0.5), math.log(8.0)))
    response = pixel_flat(key) / pixel_gain(key)
    return (intensity * response[None, :]).astype(jnp.bfloat16)


def draw_sample_frames(key, part):
    return raw_frames(key, 37)


def draw_reference_frames(key, part):
    return raw_frames(key, 41)


def draw_gain(key, part):
    return pixel_gain(key)


def draw_flat(key, part):
    return pixel_flat(key)


def with_ends(array, rng, smallest, largest):
    longest = array.shape.index(max(array.shape))
    spots = []
    for shift in (0, 1):
        where = [jax.random.randint(jax.random.fold_in(rng, axis), (), 0, length) for axis, length in enumerate(array.shape)]
        where[longest] = (where[longest] + shift) % array.shape[longest]
        spots.append(tuple(where))
    return array.at[spots[0]].set(smallest).at[spots[1]].set(largest)


def setup_inputs(seed: int = 0) -> dict:
    keys = jax.random.split(jax.random.key(seed), 8)
    sample_frames = draw_sample_frames(jax.random.fold_in(keys[7], 71), 0)
    reference_frames = draw_reference_frames(jax.random.fold_in(keys[7], 71), 0)
    gain = draw_gain(jax.random.fold_in(keys[7], 71), 0)
    flat = draw_flat(jax.random.fold_in(keys[7], 71), 0)
    qbin = with_ends(jax.random.randint(keys[4], (PIX,), 0, QBINS), jax.random.fold_in(keys[4], 1), 0, QBINS - 1).astype(jnp.int32)
    region = with_ends((jax.random.randint(keys[5], (PIX,), 0, 2) < 1).astype(jnp.int32), jax.random.fold_in(keys[5], 1), 0, 1)
    live = with_ends((jax.random.randint(keys[6], (PIX,), 0, 16) < 15).astype(jnp.int32), jax.random.fold_in(keys[6], 1), 0, 1)
    return {"sample_frames": sample_frames, "reference_frames": reference_frames, "gain": gain, "flat": flat, "qbin": qbin, "region": region, "live": live}


def reference(sample_frames, reference_frames, gain, flat, qbin, region, live):
    factor = gain / flat
    select = (qbin[None, :] == jnp.arange(QBINS, dtype=jnp.int32)[:, None]).astype(jnp.float32)
    ref_select = select * (live * (1 - region)).astype(jnp.float32)[None, :]
    counts = lax.optimization_barrier(jnp.sum(ref_select, axis=1))
    sample_weight = (live * region).astype(jnp.float32)

    def deviations(frames):
        corrected = frames.astype(jnp.float32) * factor
        sums = jnp.dot(corrected, ref_select.T, precision=lax.Precision.HIGHEST)
        means = (sums + 1.0) / (counts + 1.0)
        return corrected / means[:, qbin] - 1.0
    delta_sample = (deviations(sample_frames) * sample_weight).astype(jnp.bfloat16)
    delta_reference = deviations(reference_frames).astype(jnp.bfloat16)
    total = lax.dot_general(delta_sample.astype(jnp.float32), delta_reference.astype(jnp.float32), (((1,), (1,)), ((), ())), precision=lax.Precision.HIGHEST)
    total = total * (1.0 / math.sqrt(PIX))
    return total.reshape(FRAMES, N_ROW, N_COL, FINE)
```

```python
import math

import jax
import jax.numpy as jnp
from jax import lax
from jax.sharding import PartitionSpec as P

QBINS = 32


def _swap(x, axis):
    return lax.ppermute(x, axis, [(0, 1), (1, 0)])


def on_device(sample_frames, reference_frames, gain, flat, qbin, region, live):
    block = sample_frames.shape[0]
    n_row = lax.axis_size("row")
    n_pix = lax.axis_size("pix")
    r = lax.axis_index("row")
    p = lax.axis_index("pix")
    factor = gain / flat
    select = (qbin[None, :] == jnp.arange(QBINS, dtype=jnp.int32)[:, None]).astype(jnp.float32)
    ref_select = select * (live * (1 - region)).astype(jnp.float32)[None, :]
    sample_weight = (live * region).astype(jnp.float32)
    corrected_sample = sample_frames.astype(jnp.float32) * factor
    corrected_reference = reference_frames.astype(jnp.float32) * factor
    sums_sample = jnp.dot(corrected_sample, ref_select.T, precision=lax.Precision.HIGHEST)
    sums_reference = jnp.dot(corrected_reference, ref_select.T, precision=lax.Precision.HIGHEST)
    counts = jnp.sum(ref_select, axis=1)
    stats = (sums_sample, sums_reference, counts)
    if n_pix == 2:
        other = _swap(stats, "pix")
        stats = jax.tree.map(jnp.add, stats, other)
    else:
        stats = lax.psum(stats, "pix")
    sums_sample, sums_reference, counts = stats
    mean_sample = (sums_sample + 1.0) / (counts + 1.0)
    mean_reference = (sums_reference + 1.0) / (counts + 1.0)
    spread_sample = jnp.dot(mean_sample, select, precision=lax.Precision.HIGHEST)
    spread_reference = jnp.dot(mean_reference, select, precision=lax.Precision.HIGHEST)
    delta_sample = ((corrected_sample / spread_sample - 1.0) * sample_weight).astype(jnp.bfloat16)
    delta_reference = (corrected_reference / spread_reference - 1.0).astype(jnp.bfloat16)

    arrivals = [delta_reference]
    for k in range(1, n_row):
        perm = [(i, (i + k) % n_row) for i in range(n_row)]
        arrivals.append(lax.ppermute(delta_reference, "row", perm))

    sample_rows = lax.all_gather(delta_sample, "col", axis=0, tiled=True)
    scale = 1.0 / math.sqrt(gain.shape[0] * n_pix)
    width = block // n_pix
    out = jnp.zeros((sample_rows.shape[0], n_row, width), jnp.float32)
    for k in range(n_row):
        part = lax.dot_general(
            sample_rows,
            arrivals[k],
            (((1,), (1,)), ((), ())),
            preferred_element_type=jnp.float32,
        )
        part = part * scale
        if n_pix == 2:
            keep = lax.dynamic_slice_in_dim(part, p * width, width, 1)
            give = lax.dynamic_slice_in_dim(part, (1 - p) * width, width, 1)
            mine = keep + _swap(give, "pix")
        else:
            mine = lax.psum_scatter(part, "pix", scatter_dimension=1, tiled=True)
        a = (r - k) % n_row
        out = lax.dynamic_update_slice(out, mine[:, None, :], (0, a, 0))
    return out[:, :, None, :]


def solution(mesh):
    return jax.shard_map(
        on_device,
        mesh=mesh,
        in_specs=(
            P(("row", "col"), "pix"),
            P(("row", "col"), "pix"),
            P("pix"),
            P("pix"),
            P("pix"),
            P("pix"),
            P("pix"),
        ),
        out_specs=P("row", None, "col", "pix"),
        check_vma=False,
    )
```

```python
import math

import jax
import jax.numpy as jnp
from jax import lax
from jax.sharding import PartitionSpec as P

QBINS = 32


def _swap(x, axis):
    return lax.ppermute(x, axis, [(0, 1), (1, 0)])


def on_device(sample_frames, reference_frames, gain, flat, qbin, region, live):
    block = sample_frames.shape[0]
    n_row = lax.axis_size("row")
    n_pix = lax.axis_size("pix")
    r = lax.axis_index("row")
    p = lax.axis_index("pix")

    raw_right = [None] * n_row
    raw_left = [None] * n_row
    prev_r = reference_frames
    prev_l = reference_frames
    for s in range(1, n_row):
        prev_r = lax.ppermute(prev_r, "row", [(i, i + 1) for i in range(s - 1, n_row - 1)])
        prev_l = lax.ppermute(prev_l, "row", [(i, i - 1) for i in range(1, n_row - s + 1)])
        raw_right[s] = prev_r
        raw_left[s] = prev_l

    factor = gain / flat
    select = (qbin[None, :] == jnp.arange(QBINS, dtype=jnp.int32)[:, None]).astype(jnp.float32)
    ref_select = select * (live * (1 - region)).astype(jnp.float32)[None, :]
    sample_weight = (live * region).astype(jnp.float32)
    corrected_sample = sample_frames.astype(jnp.float32) * factor
    corrected_reference = reference_frames.astype(jnp.float32) * factor
    sums_sample = jnp.dot(corrected_sample, ref_select.T, precision=lax.Precision.HIGHEST)
    sums_reference = jnp.dot(corrected_reference, ref_select.T, precision=lax.Precision.HIGHEST)
    counts = jnp.sum(ref_select, axis=1)
    stats = (sums_sample, sums_reference, counts)
    if n_pix == 2:
        other = _swap(stats, "pix")
        stats = jax.tree.map(jnp.add, stats, other)
    else:
        stats = lax.psum(stats, "pix")
    sums_sample, sums_reference, counts = stats
    mean_sample = (sums_sample + 1.0) / (counts + 1.0)
    mean_reference = (sums_reference + 1.0) / (counts + 1.0)

    def reference_deviation(frames, mean):
        spread = jnp.dot(mean, select, precision=lax.Precision.HIGHEST)
        return (frames.astype(jnp.float32) * factor / spread - 1.0).astype(jnp.bfloat16)

    spread_sample = jnp.dot(mean_sample, select, precision=lax.Precision.HIGHEST)
    delta_sample = ((corrected_sample / spread_sample - 1.0) * sample_weight).astype(jnp.bfloat16)
    sample_rows = lax.all_gather(delta_sample, "col", axis=0, tiled=True)

    scale = 1.0 / math.sqrt(gain.shape[0] * n_pix)
    width = block // n_pix
    out = jnp.zeros((sample_rows.shape[0], n_row + 1, width), jnp.float32)

    def accumulate(out, frames, mean, slot):
        part = lax.dot_general(
            sample_rows,
            reference_deviation(frames, mean),
            (((1,), (1,)), ((), ())),
            preferred_element_type=jnp.float32,
        )
        part = part * scale
        if n_pix == 2:
            keep = lax.dynamic_slice_in_dim(part, p * width, width, 1)
            give = lax.dynamic_slice_in_dim(part, (1 - p) * width, width, 1)
            mine = keep + _swap(give, "pix")
        else:
            mine = lax.psum_scatter(part, "pix", scatter_dimension=1, tiled=True)
        return lax.dynamic_update_slice(out, mine[:, None, :], (0, slot, 0))

    out = accumulate(out, reference_frames, mean_reference, r + 1)
    for s in range(1, n_row):
        mean_r = lax.ppermute(mean_reference, "row", [(i, i + s) for i in range(n_row - s)])
        mean_l = lax.ppermute(mean_reference, "row", [(i, i - s) for i in range(s, n_row)])
        slot_r = jnp.where(r >= s, r - s + 1, 0)
        slot_l = jnp.where(r + s < n_row, r + s + 1, 0)
        out = accumulate(out, raw_right[s], mean_r, slot_r)
        out = accumulate(out, raw_left[s], mean_l, slot_l)
    return out[:, 1:, None, :]


def solution(mesh):
    return jax.shard_map(
        on_device,
        mesh=mesh,
        in_specs=(
            P(("row", "col"), "pix"),
            P(("row", "col"), "pix"),
            P("pix"),
            P("pix"),
            P("pix"),
            P("pix"),
            P("pix"),
        ),
        out_specs=P("row", None, "col", "pix"),
        check_vma=False,
    )
```

```python
import math

import jax
import jax.numpy as jnp
from jax import lax
from jax.sharding import PartitionSpec as P

QBINS = 32


def _swap(x, axis):
    return lax.ppermute(x, axis, [(0, 1), (1, 0)])


def _right(s, n):
    return [(i, i + 1) for i in range(s - 1, n - 1)]


def _left(s, n):
    return [(i, i - 1) for i in range(1, n - s + 1)]


def on_device(sample_frames, reference_frames, gain, flat, qbin, region, live):
    block = sample_frames.shape[0]
    n_row = lax.axis_size("row")
    n_pix = lax.axis_size("pix")
    r = lax.axis_index("row")
    p = lax.axis_index("pix")

    raw_rows = lax.all_gather(sample_frames, "col", axis=0, tiled=True)
    in_r = lax.ppermute(reference_frames, "row", _right(1, n_row))
    in_l = lax.ppermute(reference_frames, "row", _left(1, n_row))

    factor = gain / flat
    select = (qbin[None, :] == jnp.arange(QBINS, dtype=jnp.int32)[:, None]).astype(jnp.float32)
    ref_select = select * (live * (1 - region)).astype(jnp.float32)[None, :]
    sample_weight = (live * region).astype(jnp.float32)
    corrected_sample = sample_frames.astype(jnp.float32) * factor
    corrected_reference = reference_frames.astype(jnp.float32) * factor
    sums_sample = jnp.dot(corrected_sample, ref_select.T, precision=lax.Precision.HIGHEST)
    sums_reference = jnp.dot(corrected_reference, ref_select.T, precision=lax.Precision.HIGHEST)
    counts = jnp.sum(ref_select, axis=1)
    stats = (sums_sample, sums_reference, counts)
    if n_pix == 2:
        other = _swap(stats, "pix")
        stats = jax.tree.map(jnp.add, stats, other)
    else:
        stats = lax.psum(stats, "pix")
    sums_sample, sums_reference, counts = stats
    mean_sample = (sums_sample + 1.0) / (counts + 1.0)
    mean_reference = (sums_reference + 1.0) / (counts + 1.0)

    rows_mean = lax.all_gather(mean_sample, "col", axis=0, tiled=True)
    spread_rows = jnp.dot(rows_mean, select, precision=lax.Precision.HIGHEST)
    corrected_rows = raw_rows.astype(jnp.float32) * factor
    sample_rows = ((corrected_rows / spread_rows - 1.0) * sample_weight).astype(jnp.bfloat16)

    def reference_deviation(frames, mean):
        spread = jnp.dot(mean, select, precision=lax.Precision.HIGHEST)
        return (frames.astype(jnp.float32) * factor / spread - 1.0).astype(jnp.bfloat16)

    scale = 1.0 / math.sqrt(gain.shape[0] * n_pix)
    width = block // n_pix

    def tile(frames, mean):
        part = lax.dot_general(
            sample_rows,
            reference_deviation(frames, mean),
            (((1,), (1,)), ((), ())),
            preferred_element_type=jnp.float32,
        )
        part = part * scale
        if n_pix == 2:
            keep = lax.dynamic_slice_in_dim(part, p * width, width, 1)
            give = lax.dynamic_slice_in_dim(part, (1 - p) * width, width, 1)
            return keep + _swap(give, "pix")
        return lax.psum_scatter(part, "pix", scatter_dimension=1, tiled=True)

    tiles = [(tile(reference_frames, mean_reference), r)]
    for s in range(1, n_row):
        if s + 1 < n_row:
            nxt_r = lax.ppermute(in_r, "row", _right(s + 1, n_row))
            nxt_l = lax.ppermute(in_l, "row", _left(s + 1, n_row))
        mean_r = lax.ppermute(mean_reference, "row", [(i, i + s) for i in range(n_row - s)])
        mean_l = lax.ppermute(mean_reference, "row", [(i, i - s) for i in range(s, n_row)])
        has_r = r >= s
        has_l = r + s < n_row
        if 2 * s < n_row:
            tiles.append((tile(in_r, mean_r), jnp.where(has_r, r - s, -1)))
            tiles.append((tile(in_l, mean_l), jnp.where(has_l, r + s, -1)))
        else:
            frames = jnp.where(has_r, in_r, in_l)
            mean = jnp.where(has_r, mean_r, mean_l)
            slot = jnp.where(has_r, r - s, jnp.where(has_l, r + s, -1))
            tiles.append((tile(frames, mean), slot))
        if s + 1 < n_row:
            in_r, in_l = nxt_r, nxt_l

    slots = jnp.arange(n_row, dtype=jnp.int32)[None, :, None]
    out = jnp.zeros((sample_rows.shape[0], n_row, width), jnp.float32)
    for value, slot in tiles:
        out = jnp.where(slots == slot, value[:, None, :], out)
    return out[:, :, None, :]


def solution(mesh):
    return jax.shard_map(
        on_device,
        mesh=mesh,
        in_specs=(
            P(("row", "col"), "pix"),
            P(("row", "col"), "pix"),
            P("pix"),
            P("pix"),
            P("pix"),
            P("pix"),
            P("pix"),
        ),
        out_specs=P("row", None, "col", "pix"),
        check_vma=False,
    )
```

```python
import math

import jax
import jax.numpy as jnp
from jax import lax
from jax.sharding import PartitionSpec as P

QBINS = 32


def _swap(x, axis):
    return lax.ppermute(x, axis, [(0, 1), (1, 0)])


def _right(s, n):
    return [(i, i + 1) for i in range(s - 1, n - 1)]


def _left(s, n):
    return [(i, i - 1) for i in range(1, n - s + 1)]


def on_device(sample_frames, reference_frames, gain, flat, qbin, region, live):
    block = sample_frames.shape[0]
    n_row = lax.axis_size("row")
    n_pix = lax.axis_size("pix")
    r = lax.axis_index("row")
    p = lax.axis_index("pix")

    raw_rows = lax.all_gather(sample_frames, "col", axis=0, tiled=True)
    in_r = lax.ppermute(reference_frames, "row", _right(1, n_row))
    in_l = lax.ppermute(reference_frames, "row", _left(1, n_row))

    factor = gain / flat
    select = (qbin[None, :] == jnp.arange(QBINS, dtype=jnp.int32)[:, None]).astype(jnp.float32)
    ref_select = select * (live * (1 - region)).astype(jnp.float32)[None, :]
    sample_weight = (live * region).astype(jnp.float32)
    corrected_sample = sample_frames.astype(jnp.float32) * factor
    corrected_reference = reference_frames.astype(jnp.float32) * factor
    sums_sample = jnp.dot(corrected_sample, ref_select.T, precision=lax.Precision.HIGHEST)
    sums_reference = jnp.dot(corrected_reference, ref_select.T, precision=lax.Precision.HIGHEST)
    counts = jnp.sum(ref_select, axis=1)
    stats = (sums_sample, sums_reference, counts)
    if n_pix == 2:
        other = _swap(stats, "pix")
        stats = jax.tree.map(jnp.add, stats, other)
    else:
        stats = lax.psum(stats, "pix")
    sums_sample, sums_reference, counts = stats
    mean_sample = (sums_sample + 1.0) / (counts + 1.0)
    mean_reference = (sums_reference + 1.0) / (counts + 1.0)

    rows_mean = lax.all_gather(mean_sample, "col", axis=0, tiled=True)
    spread_rows = jnp.dot(rows_mean, select, precision=lax.Precision.HIGHEST)
    corrected_rows = raw_rows.astype(jnp.float32) * factor
    sample_rows = ((corrected_rows / spread_rows - 1.0) * sample_weight).astype(jnp.bfloat16)

    def reference_deviation(frames, mean):
        spread = jnp.dot(mean, select, precision=lax.Precision.HIGHEST)
        return (frames.astype(jnp.float32) * factor / spread - 1.0).astype(jnp.bfloat16)

    scale = 1.0 / math.sqrt(gain.shape[0] * n_pix)
    width = block // n_pix

    def tile(frames, mean):
        part = lax.dot_general(
            sample_rows,
            reference_deviation(frames, mean),
            (((1,), (1,)), ((), ())),
            preferred_element_type=jnp.float32,
        )
        part = part * scale
        if n_pix == 2:
            keep = lax.dynamic_slice_in_dim(part, p * width, width, 1)
            give = lax.dynamic_slice_in_dim(part, (1 - p) * width, width, 1)
            return keep + _swap(give, "pix")
        return lax.psum_scatter(part, "pix", scatter_dimension=1, tiled=True)

    tiles = [(tile(reference_frames, mean_reference), r)]
    for s in range(1, n_row):
        if s + 1 < n_row:
            gate = [t for t, _ in tiles] if s > 1 else []
            fwd_r, fwd_l, _ = lax.optimization_barrier((in_r, in_l, gate))
            nxt_r = lax.ppermute(fwd_r, "row", _right(s + 1, n_row))
            nxt_l = lax.ppermute(fwd_l, "row", _left(s + 1, n_row))
        mean_r = lax.ppermute(mean_reference, "row", [(i, i + s) for i in range(n_row - s)])
        mean_l = lax.ppermute(mean_reference, "row", [(i, i - s) for i in range(s, n_row)])
        has_r = r >= s
        has_l = r + s < n_row
        if 2 * s < n_row:
            tiles.append((tile(in_r, mean_r), jnp.where(has_r, r - s, -1)))
            tiles.append((tile(in_l, mean_l), jnp.where(has_l, r + s, -1)))
        else:
            frames = jnp.where(has_r, in_r, in_l)
            mean = jnp.where(has_r, mean_r, mean_l)
            slot = jnp.where(has_r, r - s, jnp.where(has_l, r + s, -1))
            tiles.append((tile(frames, mean), slot))
        if s + 1 < n_row:
            in_r, in_l = nxt_r, nxt_l

    slots = jnp.arange(n_row, dtype=jnp.int32)[None, :, None]
    out = jnp.zeros((sample_rows.shape[0], n_row, width), jnp.float32)
    for value, slot in tiles:
        out = jnp.where(slots == slot, value[:, None, :], out)
    return out[:, :, None, :]


def solution(mesh):
    return jax.shard_map(
        on_device,
        mesh=mesh,
        in_specs=(
            P(("row", "col"), "pix"),
            P(("row", "col"), "pix"),
            P("pix"),
            P("pix"),
            P("pix"),
            P("pix"),
            P("pix"),
        ),
        out_specs=P("row", None, "col", "pix"),
        check_vma=False,
    )
```

```python
import math

import jax
import jax.numpy as jnp
from jax import lax
from jax.sharding import PartitionSpec as P

QBINS = 32


def _swap(x, axis):
    return lax.ppermute(x, axis, [(0, 1), (1, 0)])


def _right(s, n):
    return [(i, i + 1) for i in range(s - 1, n - 1)]


def _left(s, n):
    return [(i, i - 1) for i in range(1, n - s + 1)]


def _bins(qbin):
    return (qbin[None, :] == jnp.arange(QBINS, dtype=jnp.int32)[:, None]).astype(jnp.float32)


def pipeline(raw_sample, raw_reference, factor_px, qbin_px, weight_px, full):
    sample_frames, reference_frames, factor, ref_select, n_total = full
    block = sample_frames.shape[0]
    n_row = lax.axis_size("row")
    n_pix = lax.axis_size("pix")
    r = lax.axis_index("row")
    p = lax.axis_index("pix")

    raw_rows = lax.all_gather(raw_sample, "col", axis=0, tiled=True)
    in_r = lax.ppermute(raw_reference, "row", _right(1, n_row))
    in_l = lax.ppermute(raw_reference, "row", _left(1, n_row))

    corrected_sample = sample_frames.astype(jnp.float32) * factor
    corrected_reference = reference_frames.astype(jnp.float32) * factor
    sums_sample = jnp.dot(corrected_sample, ref_select.T, precision=lax.Precision.HIGHEST)
    sums_reference = jnp.dot(corrected_reference, ref_select.T, precision=lax.Precision.HIGHEST)
    counts = jnp.sum(ref_select, axis=1)
    stats = (sums_sample, sums_reference, counts)
    if n_pix == 2:
        other = _swap(stats, "pix")
        stats = jax.tree.map(jnp.add, stats, other)
    else:
        stats = lax.psum(stats, "pix")
    sums_sample, sums_reference, counts = stats
    mean_sample = (sums_sample + 1.0) / (counts + 1.0)
    mean_reference = (sums_reference + 1.0) / (counts + 1.0)

    select = _bins(qbin_px)
    rows_mean = lax.all_gather(mean_sample, "col", axis=0, tiled=True)
    spread_rows = jnp.dot(rows_mean, select, precision=lax.Precision.HIGHEST)
    corrected_rows = raw_rows.astype(jnp.float32) * factor_px
    sample_rows = ((corrected_rows / spread_rows - 1.0) * weight_px).astype(jnp.bfloat16)

    def reference_deviation(frames, mean):
        spread = jnp.dot(mean, select, precision=lax.Precision.HIGHEST)
        return (frames.astype(jnp.float32) * factor_px / spread - 1.0).astype(jnp.bfloat16)

    scale = 1.0 / math.sqrt(n_total)
    width = block // n_pix

    def tile(frames, mean):
        part = lax.dot_general(
            sample_rows,
            reference_deviation(frames, mean),
            (((1,), (1,)), ((), ())),
            preferred_element_type=jnp.float32,
        )
        part = part * scale
        if n_pix == 2:
            keep = lax.dynamic_slice_in_dim(part, p * width, width, 1)
            give = lax.dynamic_slice_in_dim(part, (1 - p) * width, width, 1)
            return keep + _swap(give, "pix")
        return lax.psum_scatter(part, "pix", scatter_dimension=1, tiled=True)

    tiles = [(tile(raw_reference, mean_reference), r)]
    for s in range(1, n_row):
        if s + 1 < n_row:
            gate = [t for t, _ in tiles] if s > 1 else []
            fwd_r, fwd_l, _ = lax.optimization_barrier((in_r, in_l, gate))
            nxt_r = lax.ppermute(fwd_r, "row", _right(s + 1, n_row))
            nxt_l = lax.ppermute(fwd_l, "row", _left(s + 1, n_row))
        mean_r = lax.ppermute(mean_reference, "row", [(i, i + s) for i in range(n_row - s)])
        mean_l = lax.ppermute(mean_reference, "row", [(i, i - s) for i in range(s, n_row)])
        has_r = r >= s
        has_l = r + s < n_row
        if 2 * s < n_row:
            tiles.append((tile(in_r, mean_r), jnp.where(has_r, r - s, -1)))
            tiles.append((tile(in_l, mean_l), jnp.where(has_l, r + s, -1)))
        else:
            frames = jnp.where(has_r, in_r, in_l)
            mean = jnp.where(has_r, mean_r, mean_l)
            slot = jnp.where(has_r, r - s, jnp.where(has_l, r + s, -1))
            tiles.append((tile(frames, mean), slot))
        if s + 1 < n_row:
            in_r, in_l = nxt_r, nxt_l

    slots = jnp.arange(n_row, dtype=jnp.int32)[None, :, None]
    out = jnp.zeros((sample_rows.shape[0], n_row, width), jnp.float32)
    for value, slot in tiles:
        out = jnp.where(slots == slot, value[:, None, :], out)
    return out


def on_device(sample_frames, reference_frames, gain, flat, qbin, region, live):
    n_pix = lax.axis_size("pix")
    n_local = gain.shape[0]
    half = n_local // 2
    factor = gain / flat
    select = _bins(qbin)
    ref_select = select * (live * (1 - region)).astype(jnp.float32)[None, :]
    sample_mask = live * region
    sample_weight = sample_mask.astype(jnp.float32)
    full = (sample_frames, reference_frames, factor, ref_select, n_local * n_pix)

    count = jnp.sum(sample_mask)
    if n_pix == 2:
        widest = jnp.maximum(count, _swap(count, "pix"))
    else:
        widest = lax.pmax(count, "pix")

    def compact(operands):
        sample_frames, reference_frames = operands
        keep = sample_mask > 0
        order = jnp.cumsum(keep.astype(jnp.int32)) - 1
        target = jnp.where(keep, order, half)
        columns = jnp.zeros((half,), jnp.int32).at[target].set(
            jnp.arange(n_local, dtype=jnp.int32), mode="drop"
        )
        used = (jnp.arange(half, dtype=jnp.int32) < count).astype(jnp.float32)
        return pipeline(
            jnp.take(sample_frames, columns, axis=1),
            jnp.take(reference_frames, columns, axis=1),
            factor[columns],
            qbin[columns],
            used,
            full,
        )

    def whole(operands):
        sample_frames, reference_frames = operands
        return pipeline(sample_frames, reference_frames, factor, qbin, sample_weight, full)

    out = lax.cond(widest <= half, compact, whole, (sample_frames, reference_frames))
    return out[:, :, None, :]


def solution(mesh):
    return jax.shard_map(
        on_device,
        mesh=mesh,
        in_specs=(
            P(("row", "col"), "pix"),
            P(("row", "col"), "pix"),
            P("pix"),
            P("pix"),
            P("pix"),
            P("pix"),
            P("pix"),
        ),
        out_specs=P("row", None, "col", "pix"),
        check_vma=False,
    )
```

```python
import math

import jax
import jax.numpy as jnp
from jax import lax
from jax.sharding import PartitionSpec as P

QBINS = 32


def _swap(x, axis):
    return lax.ppermute(x, axis, [(0, 1), (1, 0)])


def _right(s, n):
    return [(i, i + 1) for i in range(s - 1, n - 1)]


def _left(s, n):
    return [(i, i - 1) for i in range(1, n - s + 1)]


def _bins(qbin):
    return (qbin[None, :] == jnp.arange(QBINS, dtype=jnp.int32)[:, None]).astype(jnp.float32)


def pipeline(raw_sample, raw_reference, factor_px, qbin_px, weight_px, full):
    sample_frames, reference_frames, factor, ref_select, n_total = full
    block = sample_frames.shape[0]
    n_row = lax.axis_size("row")
    n_pix = lax.axis_size("pix")
    r = lax.axis_index("row")
    p = lax.axis_index("pix")

    raw_rows = lax.all_gather(raw_sample, "col", axis=0, tiled=True)
    in_r = lax.ppermute(raw_reference, "row", _right(1, n_row))
    in_l = lax.ppermute(raw_reference, "row", _left(1, n_row))

    corrected_sample = sample_frames.astype(jnp.float32) * factor
    corrected_reference = reference_frames.astype(jnp.float32) * factor
    sums_sample = jnp.dot(corrected_sample, ref_select.T, precision=lax.Precision.HIGHEST)
    sums_reference = jnp.dot(corrected_reference, ref_select.T, precision=lax.Precision.HIGHEST)
    counts = jnp.sum(ref_select, axis=1)
    stats = (sums_sample, sums_reference, counts)
    if n_pix == 2:
        other = _swap(stats, "pix")
        stats = jax.tree.map(jnp.add, stats, other)
    else:
        stats = lax.psum(stats, "pix")
    sums_sample, sums_reference, counts = stats
    mean_sample = (sums_sample + 1.0) / (counts + 1.0)
    mean_reference = (sums_reference + 1.0) / (counts + 1.0)

    select = _bins(qbin_px)
    rows_mean = lax.all_gather(mean_sample, "col", axis=0, tiled=True)
    spread_rows = jnp.dot(rows_mean, select, precision=lax.Precision.HIGHEST)
    corrected_rows = raw_rows.astype(jnp.float32) * factor_px
    sample_rows = ((corrected_rows / spread_rows - 1.0) * weight_px).astype(jnp.bfloat16)

    def reference_deviation(frames, mean):
        spread = jnp.dot(mean, select, precision=lax.Precision.HIGHEST)
        return (frames.astype(jnp.float32) * factor_px / spread - 1.0).astype(jnp.bfloat16)

    scale = 1.0 / math.sqrt(n_total)
    width = block // n_pix

    def tile(frames, mean):
        part = lax.dot_general(
            sample_rows,
            reference_deviation(frames, mean),
            (((1,), (1,)), ((), ())),
            preferred_element_type=jnp.float32,
        )
        part = part * scale
        if n_pix == 2:
            keep = lax.dynamic_slice_in_dim(part, p * width, width, 1)
            give = lax.dynamic_slice_in_dim(part, (1 - p) * width, width, 1)
            return keep + _swap(give, "pix")
        return lax.psum_scatter(part, "pix", scatter_dimension=1, tiled=True)

    tiles = [(tile(raw_reference, mean_reference), r)]
    for s in range(1, n_row):
        if s + 1 < n_row:
            gate = [t for t, _ in tiles] if s > 1 else []
            fwd_r, fwd_l, _ = lax.optimization_barrier((in_r, in_l, gate))
            nxt_r = lax.ppermute(fwd_r, "row", _right(s + 1, n_row))
            nxt_l = lax.ppermute(fwd_l, "row", _left(s + 1, n_row))
        mean_r = lax.ppermute(mean_reference, "row", [(i, i + s) for i in range(n_row - s)])
        mean_l = lax.ppermute(mean_reference, "row", [(i, i - s) for i in range(s, n_row)])
        has_r = r >= s
        has_l = r + s < n_row
        if 2 * s < n_row:
            tiles.append((tile(in_r, mean_r), jnp.where(has_r, r - s, -1)))
            tiles.append((tile(in_l, mean_l), jnp.where(has_l, r + s, -1)))
        else:
            frames = jnp.where(has_r, in_r, in_l)
            mean = jnp.where(has_r, mean_r, mean_l)
            slot = jnp.where(has_r, r - s, jnp.where(has_l, r + s, -1))
            tiles.append((tile(frames, mean), slot))
        if s + 1 < n_row:
            in_r, in_l = nxt_r, nxt_l

    slots = jnp.arange(n_row, dtype=jnp.int32)[None, :, None]
    out = jnp.zeros((sample_rows.shape[0], n_row, width), jnp.float32)
    for value, slot in tiles:
        out = jnp.where(slots == slot, value[:, None, :], out)
    return out


def on_device(sample_frames, reference_frames, gain, flat, qbin, region, live):
    n_pix = lax.axis_size("pix")
    n_local = gain.shape[0]
    factor = gain / flat
    select = _bins(qbin)
    ref_select = select * (live * (1 - region)).astype(jnp.float32)[None, :]
    sample_mask = live * region
    sample_weight = sample_mask.astype(jnp.float32)
    full = (sample_frames, reference_frames, factor, ref_select, n_local * n_pix)

    n_chunk = 4 if n_local % 8 == 0 else 1
    chunk = n_local // n_chunk
    slots = chunk // 2
    keep = (sample_mask > 0).reshape(n_chunk, chunk)
    count = jnp.sum(keep.astype(jnp.int32), axis=1)
    if n_pix == 2:
        widest = jnp.max(jnp.maximum(count, _swap(count, "pix")))
    else:
        widest = lax.pmax(jnp.max(count), "pix")

    def compact(operands):
        sample_frames, reference_frames = operands
        order = jnp.cumsum(keep.astype(jnp.int32), axis=1) - 1
        picks = keep[:, :, None] & (order[:, :, None] == jnp.arange(slots, dtype=jnp.int32)[None, None, :])
        picks = picks.astype(jnp.bfloat16)

        def cut(frames):
            pieces = [
                jnp.dot(frames[:, i * chunk:(i + 1) * chunk], picks[i], preferred_element_type=jnp.float32)
                for i in range(n_chunk)
            ]
            return jnp.concatenate(pieces, axis=1).astype(frames.dtype)

        table = jnp.stack([factor, qbin.astype(jnp.float32)])
        table = jnp.concatenate(
            [jnp.dot(table[:, i * chunk:(i + 1) * chunk], picks[i].astype(jnp.float32),
                     precision=lax.Precision.HIGHEST) for i in range(n_chunk)],
            axis=1,
        )
        used = (jnp.arange(slots, dtype=jnp.int32)[None, :] < count[:, None]).astype(jnp.float32)
        return pipeline(
            cut(sample_frames),
            cut(reference_frames),
            table[0],
            table[1].astype(jnp.int32),
            used.reshape(-1),
            full,
        )

    def whole(operands):
        sample_frames, reference_frames = operands
        return pipeline(sample_frames, reference_frames, factor, qbin, sample_weight, full)

    out = lax.cond(widest <= slots, compact, whole, (sample_frames, reference_frames))
    return out[:, :, None, :]


def solution(mesh):
    return jax.shard_map(
        on_device,
        mesh=mesh,
        in_specs=(
            P(("row", "col"), "pix"),
            P(("row", "col"), "pix"),
            P("pix"),
            P("pix"),
            P("pix"),
            P("pix"),
            P("pix"),
        ),
        out_specs=P("row", None, "col", "pix"),
        check_vma=False,
    )
```

```python
import math

import jax
import jax.numpy as jnp
from jax import lax
from jax.sharding import PartitionSpec as P

QBINS = 32


def _swap(x, axis):
    return lax.ppermute(x, axis, [(0, 1), (1, 0)])


def _right(s, n):
    return [(i, i + 1) for i in range(s - 1, n - 1)]


def _left(s, n):
    return [(i, i - 1) for i in range(1, n - s + 1)]


def _bins(qbin):
    return (qbin[None, :] == jnp.arange(QBINS, dtype=jnp.int32)[:, None]).astype(jnp.float32)


def pipeline(raw_sample, raw_reference, factor_px, qbin_px, weight_px, full):
    sample_frames, reference_frames, factor, ref_select, n_total = full
    block = sample_frames.shape[0]
    n_row = lax.axis_size("row")
    n_pix = lax.axis_size("pix")
    r = lax.axis_index("row")
    p = lax.axis_index("pix")

    raw_rows = lax.all_gather(raw_sample, "col", axis=0, tiled=True)
    in_r = lax.ppermute(raw_reference, "row", _right(1, n_row))
    in_l = lax.ppermute(raw_reference, "row", _left(1, n_row))

    corrected_sample = sample_frames.astype(jnp.float32) * factor
    corrected_reference = reference_frames.astype(jnp.float32) * factor
    sums_sample = jnp.dot(corrected_sample, ref_select.T, precision=lax.Precision.HIGHEST)
    sums_reference = jnp.dot(corrected_reference, ref_select.T, precision=lax.Precision.HIGHEST)
    counts = jnp.sum(ref_select, axis=1)
    stats = (sums_sample, sums_reference, counts)
    if n_pix == 2:
        other = _swap(stats, "pix")
        stats = jax.tree.map(jnp.add, stats, other)
    else:
        stats = lax.psum(stats, "pix")
    sums_sample, sums_reference, counts = stats
    mean_sample = (sums_sample + 1.0) / (counts + 1.0)
    mean_reference = (sums_reference + 1.0) / (counts + 1.0)

    select = _bins(qbin_px)
    rows_mean = lax.all_gather(mean_sample, "col", axis=0, tiled=True)
    spread_rows = jnp.dot(rows_mean, select, precision=lax.Precision.HIGHEST)
    corrected_rows = raw_rows.astype(jnp.float32) * factor_px
    sample_rows = ((corrected_rows / spread_rows - 1.0) * weight_px).astype(jnp.bfloat16)

    def reference_deviation(frames, mean):
        spread = jnp.dot(mean, select, precision=lax.Precision.HIGHEST)
        return (frames.astype(jnp.float32) * factor_px / spread - 1.0).astype(jnp.bfloat16)

    scale = 1.0 / math.sqrt(n_total)
    width = block // n_pix

    def tile(frames, mean):
        part = lax.dot_general(
            sample_rows,
            reference_deviation(frames, mean),
            (((1,), (1,)), ((), ())),
            preferred_element_type=jnp.float32,
        )
        part = part * scale
        if n_pix == 2:
            keep = lax.dynamic_slice_in_dim(part, p * width, width, 1)
            give = lax.dynamic_slice_in_dim(part, (1 - p) * width, width, 1)
            return keep + _swap(give, "pix")
        return lax.psum_scatter(part, "pix", scatter_dimension=1, tiled=True)

    tiles = [(tile(raw_reference, mean_reference), r)]
    for s in range(1, n_row):
        if s + 1 < n_row:
            gate = [t for t, _ in tiles] if s > 1 else []
            fwd_r, fwd_l, _ = lax.optimization_barrier((in_r, in_l, gate))
            nxt_r = lax.ppermute(fwd_r, "row", _right(s + 1, n_row))
            nxt_l = lax.ppermute(fwd_l, "row", _left(s + 1, n_row))
        mean_r = lax.ppermute(mean_reference, "row", [(i, i + s) for i in range(n_row - s)])
        mean_l = lax.ppermute(mean_reference, "row", [(i, i - s) for i in range(s, n_row)])
        has_r = r >= s
        has_l = r + s < n_row
        if 2 * s < n_row:
            tiles.append((tile(in_r, mean_r), jnp.where(has_r, r - s, -1)))
            tiles.append((tile(in_l, mean_l), jnp.where(has_l, r + s, -1)))
        else:
            frames = jnp.where(has_r, in_r, in_l)
            mean = jnp.where(has_r, mean_r, mean_l)
            slot = jnp.where(has_r, r - s, jnp.where(has_l, r + s, -1))
            tiles.append((tile(frames, mean), slot))
        if s + 1 < n_row:
            in_r, in_l = nxt_r, nxt_l

    slots = jnp.arange(n_row, dtype=jnp.int32)[None, :, None]
    out = jnp.zeros((sample_rows.shape[0], n_row, width), jnp.float32)
    for value, slot in tiles[:-1]:
        out = jnp.where(slots == slot, value[:, None, :], out)
    value, slot = tiles[-1]
    out = lax.optimization_barrier(out)
    return jnp.where(slots == slot, value[:, None, :], out)


def on_device(sample_frames, reference_frames, gain, flat, qbin, region, live):
    n_pix = lax.axis_size("pix")
    n_local = gain.shape[0]
    factor = gain / flat
    select = _bins(qbin)
    ref_select = select * (live * (1 - region)).astype(jnp.float32)[None, :]
    sample_mask = live * region
    sample_weight = sample_mask.astype(jnp.float32)
    full = (sample_frames, reference_frames, factor, ref_select, n_local * n_pix)

    n_chunk = 4 if n_local % 8 == 0 else 1
    chunk = n_local // n_chunk
    slots = chunk // 2
    keep = (sample_mask > 0).reshape(n_chunk, chunk)
    count = jnp.sum(keep.astype(jnp.int32), axis=1)
    if n_pix == 2:
        widest = jnp.max(jnp.maximum(count, _swap(count, "pix")))
    else:
        widest = lax.pmax(jnp.max(count), "pix")

    order = jnp.cumsum(keep.astype(jnp.int32), axis=1) - 1
    picks = keep[:, :, None] & (order[:, :, None] == jnp.arange(slots, dtype=jnp.int32)[None, None, :])
    picks = picks.astype(jnp.bfloat16)

    def cut(frames):
        pieces = [
            jnp.dot(frames[:, i * chunk:(i + 1) * chunk], picks[i], preferred_element_type=jnp.float32)
            for i in range(n_chunk)
        ]
        return jnp.concatenate(pieces, axis=1).astype(frames.dtype)

    table = jnp.stack([factor, qbin.astype(jnp.float32)])
    table = jnp.concatenate(
        [jnp.dot(table[:, i * chunk:(i + 1) * chunk], picks[i].astype(jnp.float32),
                 precision=lax.Precision.HIGHEST) for i in range(n_chunk)],
        axis=1,
    )
    used = (jnp.arange(slots, dtype=jnp.int32)[None, :] < count[:, None]).astype(jnp.float32)
    cut_operands = (cut(sample_frames), cut(reference_frames), table, used.reshape(-1))

    def compact(operands):
        cut_sample, cut_reference, table, used = operands[2]
        return pipeline(cut_sample, cut_reference, table[0], table[1].astype(jnp.int32), used, full)

    def whole(operands):
        sample_frames, reference_frames, _ = operands
        return pipeline(sample_frames, reference_frames, factor, qbin, sample_weight, full)

    out = lax.cond(widest <= slots, compact, whole, (sample_frames, reference_frames, cut_operands))
    return out[:, :, None, :]


def solution(mesh):
    return jax.shard_map(
        on_device,
        mesh=mesh,
        in_specs=(
            P(("row", "col"), "pix"),
            P(("row", "col"), "pix"),
            P("pix"),
            P("pix"),
            P("pix"),
            P("pix"),
            P("pix"),
        ),
        out_specs=P("row", None, "col", "pix"),
        check_vma=False,
    )
```

```python
import math

import jax
import jax.numpy as jnp
from jax import lax
from jax.sharding import PartitionSpec as P

QBINS = 32


def _swap(x, axis):
    return lax.ppermute(x, axis, [(0, 1), (1, 0)])


def _right(s, n):
    return [(i, i + 1) for i in range(s - 1, n - 1)]


def _left(s, n):
    return [(i, i - 1) for i in range(1, n - s + 1)]


def _bins(qbin):
    return (qbin[None, :] == jnp.arange(QBINS, dtype=jnp.int32)[:, None]).astype(jnp.float32)


def finish(raw_rows, own, in_r, in_l, factor_px, qbin_px, weight_px, means, n_total):
    rows_mean, mean_reference, mean_right, mean_left = means
    block = own.shape[0]
    n_row = lax.axis_size("row")
    n_pix = lax.axis_size("pix")
    r = lax.axis_index("row")
    p = lax.axis_index("pix")

    select = _bins(qbin_px)
    spread_rows = jnp.dot(rows_mean, select, precision=lax.Precision.HIGHEST)
    corrected_rows = raw_rows.astype(jnp.float32) * factor_px
    sample_rows = ((corrected_rows / spread_rows - 1.0) * weight_px).astype(jnp.bfloat16)

    def reference_deviation(frames, mean):
        spread = jnp.dot(mean, select, precision=lax.Precision.HIGHEST)
        return (frames.astype(jnp.float32) * factor_px / spread - 1.0).astype(jnp.bfloat16)

    scale = 1.0 / math.sqrt(n_total)
    width = block // n_pix

    def tile(frames, mean):
        part = lax.dot_general(
            sample_rows,
            reference_deviation(frames, mean),
            (((1,), (1,)), ((), ())),
            preferred_element_type=jnp.float32,
        )
        part = part * scale
        if n_pix == 2:
            keep = lax.dynamic_slice_in_dim(part, p * width, width, 1)
            give = lax.dynamic_slice_in_dim(part, (1 - p) * width, width, 1)
            return keep + _swap(give, "pix")
        return lax.psum_scatter(part, "pix", scatter_dimension=1, tiled=True)

    tiles = [(tile(own, mean_reference), r)]
    for s in range(1, n_row):
        if s + 1 < n_row:
            gate = [t for t, _ in tiles] if s > 1 else []
            fwd_r, fwd_l, _ = lax.optimization_barrier((in_r, in_l, gate))
            nxt_r = lax.ppermute(fwd_r, "row", _right(s + 1, n_row))
            nxt_l = lax.ppermute(fwd_l, "row", _left(s + 1, n_row))
        mean_r = mean_right[s - 1]
        mean_l = mean_left[s - 1]
        has_r = r >= s
        has_l = r + s < n_row
        if 2 * s < n_row:
            tiles.append((tile(in_r, mean_r), jnp.where(has_r, r - s, -1)))
            tiles.append((tile(in_l, mean_l), jnp.where(has_l, r + s, -1)))
        else:
            frames = jnp.where(has_r, in_r, in_l)
            mean = jnp.where(has_r, mean_r, mean_l)
            slot = jnp.where(has_r, r - s, jnp.where(has_l, r + s, -1))
            tiles.append((tile(frames, mean), slot))
        if s + 1 < n_row:
            in_r, in_l = nxt_r, nxt_l

    slots = jnp.arange(n_row, dtype=jnp.int32)[None, :, None]
    out = jnp.zeros((sample_rows.shape[0], n_row, width), jnp.float32)
    for value, slot in tiles[:-1]:
        out = jnp.where(slots == slot, value[:, None, :], out)
    value, slot = tiles[-1]
    out = lax.optimization_barrier(out)
    return jnp.where(slots == slot, value[:, None, :], out)


def first_hops(sample_frames, reference_frames):
    n_row = lax.axis_size("row")
    raw_rows = lax.all_gather(sample_frames, "col", axis=0, tiled=True)
    in_r = lax.ppermute(reference_frames, "row", _right(1, n_row))
    in_l = lax.ppermute(reference_frames, "row", _left(1, n_row))
    return raw_rows, in_r, in_l


def on_device(sample_frames, reference_frames, gain, flat, qbin, region, live):
    n_pix = lax.axis_size("pix")
    n_row = lax.axis_size("row")
    n_local = gain.shape[0]
    n_total = n_local * n_pix
    factor = gain / flat
    select = _bins(qbin)
    ref_select = select * (live * (1 - region)).astype(jnp.float32)[None, :]
    sample_mask = live * region
    sample_weight = sample_mask.astype(jnp.float32)

    n_chunk = 4 if n_local % 8 == 0 else 1
    chunk = n_local // n_chunk
    slots = chunk // 2
    keep = (sample_mask > 0).reshape(n_chunk, chunk)
    count = jnp.sum(keep.astype(jnp.int32), axis=1)
    if n_pix == 2:
        widest = jnp.max(jnp.maximum(count, _swap(count, "pix")))
    else:
        widest = lax.pmax(jnp.max(count), "pix")

    order = jnp.cumsum(keep.astype(jnp.int32), axis=1) - 1
    picks = keep[:, :, None] & (order[:, :, None] == jnp.arange(slots, dtype=jnp.int32)[None, None, :])
    picks = picks.astype(jnp.bfloat16)

    def cut(frames):
        pieces = [
            jnp.dot(frames[:, i * chunk:(i + 1) * chunk], picks[i], preferred_element_type=jnp.float32)
            for i in range(n_chunk)
        ]
        return jnp.concatenate(pieces, axis=1).astype(frames.dtype)

    cut_sample = cut(sample_frames)
    cut_reference = cut(reference_frames)
    cut_hops = first_hops(cut_sample, cut_reference)
    table = jnp.stack([factor, qbin.astype(jnp.float32)])
    table = jnp.concatenate(
        [jnp.dot(table[:, i * chunk:(i + 1) * chunk], picks[i].astype(jnp.float32),
                 precision=lax.Precision.HIGHEST) for i in range(n_chunk)],
        axis=1,
    )
    used = (jnp.arange(slots, dtype=jnp.int32)[None, :] < count[:, None]).astype(jnp.float32).reshape(-1)

    corrected_sample = sample_frames.astype(jnp.float32) * factor
    corrected_reference = reference_frames.astype(jnp.float32) * factor
    sums_sample = jnp.dot(corrected_sample, ref_select.T, precision=lax.Precision.HIGHEST)
    sums_reference = jnp.dot(corrected_reference, ref_select.T, precision=lax.Precision.HIGHEST)
    counts = jnp.sum(ref_select, axis=1)
    stats = (sums_sample, sums_reference, counts)
    if n_pix == 2:
        other = _swap(stats, "pix")
        stats = jax.tree.map(jnp.add, stats, other)
    else:
        stats = lax.psum(stats, "pix")
    sums_sample, sums_reference, counts = stats
    mean_sample = (sums_sample + 1.0) / (counts + 1.0)
    mean_reference = (sums_reference + 1.0) / (counts + 1.0)
    rows_mean = lax.all_gather(mean_sample, "col", axis=0, tiled=True)
    mean_right = [lax.ppermute(mean_reference, "row", [(i, i + s) for i in range(n_row - s)])
                  for s in range(1, n_row)]
    mean_left = [lax.ppermute(mean_reference, "row", [(i, i - s) for i in range(s, n_row)])
                 for s in range(1, n_row)]
    means = (rows_mean, mean_reference, mean_right, mean_left)

    def compact(operands):
        _, _, hops, cut_reference, table, used, means = operands
        raw_rows, in_r, in_l = hops
        return finish(raw_rows, cut_reference, in_r, in_l, table[0], table[1].astype(jnp.int32), used,
                      means, n_total)

    def whole(operands):
        sample_frames, reference_frames, _, _, _, _, means = operands
        raw_rows, in_r, in_l = first_hops(sample_frames, reference_frames)
        return finish(raw_rows, reference_frames, in_r, in_l, factor, qbin, sample_weight, means, n_total)

    operands = (sample_frames, reference_frames, cut_hops, cut_reference, table, used, means)
    out = lax.cond(widest <= slots, compact, whole, operands)
    return out[:, :, None, :]


def solution(mesh):
    return jax.shard_map(
        on_device,
        mesh=mesh,
        in_specs=(
            P(("row", "col"), "pix"),
            P(("row", "col"), "pix"),
            P("pix"),
            P("pix"),
            P("pix"),
            P("pix"),
            P("pix"),
        ),
        out_specs=P("row", None, "col", "pix"),
        check_vma=False,
    )
```

```python
import math

import jax
import jax.numpy as jnp
from jax import lax
from jax.sharding import PartitionSpec as P

QBINS = 32


def _swap(x, axis):
    return lax.ppermute(x, axis, [(0, 1), (1, 0)])


def _right(s, n):
    return [(i, i + 1) for i in range(s - 1, n - 1)]


def _left(s, n):
    return [(i, i - 1) for i in range(1, n - s + 1)]


def _bins(qbin):
    return (qbin[None, :] == jnp.arange(QBINS, dtype=jnp.int32)[:, None]).astype(jnp.float32)


def pipeline(raw_sample, raw_reference, factor_px, qbin_px, weight_px, full):
    sample_frames, reference_frames, factor, ref_select, n_total = full
    block = sample_frames.shape[0]
    n_row = lax.axis_size("row")
    n_pix = lax.axis_size("pix")
    r = lax.axis_index("row")
    p = lax.axis_index("pix")

    raw_rows = lax.all_gather(raw_sample, "col", axis=0, tiled=True)
    in_r = lax.ppermute(raw_reference, "row", _right(1, n_row))
    in_l = lax.ppermute(raw_reference, "row", _left(1, n_row))

    corrected_sample = sample_frames.astype(jnp.float32) * factor
    corrected_reference = reference_frames.astype(jnp.float32) * factor
    sums_sample = jnp.dot(corrected_sample, ref_select.T, precision=lax.Precision.HIGHEST)
    sums_reference = jnp.dot(corrected_reference, ref_select.T, precision=lax.Precision.HIGHEST)
    counts = jnp.sum(ref_select, axis=1)
    stats = (sums_sample, sums_reference, counts)
    if n_pix == 2:
        other = _swap(stats, "pix")
        stats = jax.tree.map(jnp.add, stats, other)
    else:
        stats = lax.psum(stats, "pix")
    sums_sample, sums_reference, counts = stats
    mean_sample = (sums_sample + 1.0) / (counts + 1.0)
    mean_reference = (sums_reference + 1.0) / (counts + 1.0)

    select = _bins(qbin_px)
    rows_mean = lax.all_gather(mean_sample, "col", axis=0, tiled=True)
    spread_rows = jnp.dot(rows_mean, select, precision=lax.Precision.HIGHEST)
    corrected_rows = raw_rows.astype(jnp.float32) * factor_px
    sample_rows = ((corrected_rows / spread_rows - 1.0) * weight_px).astype(jnp.bfloat16)

    def reference_deviation(frames, mean):
        spread = jnp.dot(mean, select, precision=lax.Precision.HIGHEST)
        return (frames.astype(jnp.float32) * factor_px / spread - 1.0).astype(jnp.bfloat16)

    scale = 1.0 / math.sqrt(n_total)
    width = block // n_pix

    def tile(frames, mean):
        part = lax.dot_general(
            sample_rows,
            reference_deviation(frames, mean),
            (((1,), (1,)), ((), ())),
            preferred_element_type=jnp.float32,
        )
        part = part * scale
        if n_pix == 2:
            keep = lax.dynamic_slice_in_dim(part, p * width, width, 1)
            give = lax.dynamic_slice_in_dim(part, (1 - p) * width, width, 1)
            return keep + _swap(give, "pix")
        return lax.psum_scatter(part, "pix", scatter_dimension=1, tiled=True)

    tiles = [(tile(raw_reference, mean_reference), r)]
    for s in range(1, n_row):
        if s + 1 < n_row:
            gate = [t for t, _ in tiles] if s > 1 else []
            fwd_r, fwd_l, _ = lax.optimization_barrier((in_r, in_l, gate))
            nxt_r = lax.ppermute(fwd_r, "row", _right(s + 1, n_row))
            nxt_l = lax.ppermute(fwd_l, "row", _left(s + 1, n_row))
        mean_r = lax.ppermute(mean_reference, "row", [(i, i + s) for i in range(n_row - s)])
        mean_l = lax.ppermute(mean_reference, "row", [(i, i - s) for i in range(s, n_row)])
        has_r = r >= s
        has_l = r + s < n_row
        if 2 * s < n_row:
            tiles.append((tile(in_r, mean_r), jnp.where(has_r, r - s, -1)))
            tiles.append((tile(in_l, mean_l), jnp.where(has_l, r + s, -1)))
        else:
            frames = jnp.where(has_r, in_r, in_l)
            mean = jnp.where(has_r, mean_r, mean_l)
            slot = jnp.where(has_r, r - s, jnp.where(has_l, r + s, -1))
            tiles.append((tile(frames, mean), slot))
        if s + 1 < n_row:
            in_r, in_l = nxt_r, nxt_l

    slots = jnp.arange(n_row, dtype=jnp.int32)[None, :, None]
    out = jnp.zeros((sample_rows.shape[0], n_row, width), jnp.float32)
    for value, slot in tiles[:-1]:
        out = jnp.where(slots == slot, value[:, None, :], out)
    value, slot = tiles[-1]
    out = lax.optimization_barrier(out)
    return jnp.where(slots == slot, value[:, None, :], out)


def on_device(sample_frames, reference_frames, gain, flat, qbin, region, live):
    n_pix = lax.axis_size("pix")
    n_local = gain.shape[0]
    factor = gain / flat
    select = _bins(qbin)
    ref_select = select * (live * (1 - region)).astype(jnp.float32)[None, :]
    sample_mask = live * region
    sample_weight = sample_mask.astype(jnp.float32)
    full = (sample_frames, reference_frames, factor, ref_select, n_local * n_pix)

    n_chunk = 4 if n_local % 8 == 0 else 1
    chunk = n_local // n_chunk
    slots = chunk // 2
    keep = (sample_mask > 0).reshape(n_chunk, chunk)
    count = jnp.sum(keep.astype(jnp.int32), axis=1)
    if n_pix == 2:
        widest = jnp.max(jnp.maximum(count, _swap(count, "pix")))
    else:
        widest = lax.pmax(jnp.max(count), "pix")

    order = jnp.cumsum(keep.astype(jnp.int32), axis=1) - 1
    picks = keep[:, :, None] & (order[:, :, None] == jnp.arange(slots, dtype=jnp.int32)[None, None, :])
    picks = picks.astype(jnp.bfloat16)

    def cut(frames):
        pieces = [
            jnp.dot(frames[:, i * chunk:(i + 1) * chunk], picks[i], preferred_element_type=jnp.float32)
            for i in range(n_chunk)
        ]
        return jnp.concatenate(pieces, axis=1).astype(frames.dtype)

    used = (jnp.arange(slots, dtype=jnp.int32)[None, :] < count[:, None]).astype(jnp.float32)
    cut_operands = (cut(sample_frames), cut(reference_frames), picks, used.reshape(-1))

    def compact(operands):
        cut_sample, cut_reference, picks, used = operands[2]
        table = jnp.stack([factor, qbin.astype(jnp.float32)])
        table = jnp.concatenate(
            [jnp.dot(table[:, i * chunk:(i + 1) * chunk], picks[i].astype(jnp.float32),
                     precision=lax.Precision.HIGHEST) for i in range(n_chunk)],
            axis=1,
        )
        return pipeline(cut_sample, cut_reference, table[0], table[1].astype(jnp.int32), used, full)

    def whole(operands):
        sample_frames, reference_frames, _ = operands
        return pipeline(sample_frames, reference_frames, factor, qbin, sample_weight, full)

    out = lax.cond(widest <= slots, compact, whole, (sample_frames, reference_frames, cut_operands))
    return out[:, :, None, :]


def solution(mesh):
    return jax.shard_map(
        on_device,
        mesh=mesh,
        in_specs=(
            P(("row", "col"), "pix"),
            P(("row", "col"), "pix"),
            P("pix"),
            P("pix"),
            P("pix"),
            P("pix"),
            P("pix"),
        ),
        out_specs=P("row", None, "col", "pix"),
        check_vma=False,
    )
```

```python
import math

import jax
import jax.numpy as jnp
from jax import lax
from jax.sharding import PartitionSpec as P

QBINS = 32


def _swap(x, axis):
    return lax.ppermute(x, axis, [(0, 1), (1, 0)])


def _right(s, n):
    return [(i, i + 1) for i in range(s - 1, n - 1)]


def _left(s, n):
    return [(i, i - 1) for i in range(1, n - s + 1)]


def _bins(qbin):
    return (qbin[None, :] == jnp.arange(QBINS, dtype=jnp.int32)[:, None]).astype(jnp.float32)


def pipeline(raw_sample, raw_reference, factor_px, qbin_px, weight_px, full):
    sample_frames, reference_frames, factor, ref_select, n_total = full
    block = sample_frames.shape[0]
    n_row = lax.axis_size("row")
    n_pix = lax.axis_size("pix")
    r = lax.axis_index("row")
    p = lax.axis_index("pix")

    raw_rows = lax.all_gather(raw_sample, "col", axis=0, tiled=True)
    in_r = lax.ppermute(raw_reference, "row", _right(1, n_row))
    in_l = lax.ppermute(raw_reference, "row", _left(1, n_row))

    corrected_sample = sample_frames.astype(jnp.float32) * factor
    corrected_reference = reference_frames.astype(jnp.float32) * factor
    sums_sample = jnp.dot(corrected_sample, ref_select.T, precision=lax.Precision.HIGHEST)
    sums_reference = jnp.dot(corrected_reference, ref_select.T, precision=lax.Precision.HIGHEST)
    counts = jnp.sum(ref_select, axis=1)
    stats = (sums_sample, sums_reference, counts)
    if n_pix == 2:
        other = _swap(stats, "pix")
        stats = jax.tree.map(jnp.add, stats, other)
    else:
        stats = lax.psum(stats, "pix")
    sums_sample, sums_reference, counts = stats
    mean_sample = (sums_sample + 1.0) / (counts + 1.0)
    mean_reference = (sums_reference + 1.0) / (counts + 1.0)

    select = _bins(qbin_px)
    rows_mean = lax.all_gather(mean_sample, "col", axis=0, tiled=True)
    spread_rows = jnp.dot(rows_mean, select, precision=lax.Precision.HIGHEST)
    corrected_rows = raw_rows.astype(jnp.float32) * factor_px
    sample_rows = ((corrected_rows / spread_rows - 1.0) * weight_px).astype(jnp.bfloat16)

    def reference_deviation(frames, mean):
        spread = jnp.dot(mean, select, precision=lax.Precision.HIGHEST)
        return (frames.astype(jnp.float32) * factor_px / spread - 1.0).astype(jnp.bfloat16)

    scale = 1.0 / math.sqrt(n_total)
    width = block // n_pix

    def tile(frames, mean):
        part = lax.dot_general(
            sample_rows,
            reference_deviation(frames, mean),
            (((1,), (1,)), ((), ())),
            preferred_element_type=jnp.float32,
        )
        part = part * scale
        if n_pix == 2:
            keep = lax.dynamic_slice_in_dim(part, p * width, width, 1)
            give = lax.dynamic_slice_in_dim(part, (1 - p) * width, width, 1)
            return keep + _swap(give, "pix")
        return lax.psum_scatter(part, "pix", scatter_dimension=1, tiled=True)

    tiles = [(tile(raw_reference, mean_reference), r)]
    for s in range(1, n_row):
        if s + 1 < n_row:
            gate = [t for t, _ in tiles] if s > 1 else []
            fwd_r, fwd_l, _ = lax.optimization_barrier((in_r, in_l, gate))
            nxt_r = lax.ppermute(fwd_r, "row", _right(s + 1, n_row))
            nxt_l = lax.ppermute(fwd_l, "row", _left(s + 1, n_row))
        mean_r = lax.ppermute(mean_reference, "row", [(i, i + s) for i in range(n_row - s)])
        mean_l = lax.ppermute(mean_reference, "row", [(i, i - s) for i in range(s, n_row)])
        has_r = r >= s
        has_l = r + s < n_row
        if 2 * s < n_row:
            tiles.append((tile(in_r, mean_r), jnp.where(has_r, r - s, -1)))
            tiles.append((tile(in_l, mean_l), jnp.where(has_l, r + s, -1)))
        else:
            frames = jnp.where(has_r, in_r, in_l)
            mean = jnp.where(has_r, mean_r, mean_l)
            slot = jnp.where(has_r, r - s, jnp.where(has_l, r + s, -1))
            tiles.append((tile(frames, mean), slot))
        if s + 1 < n_row:
            in_r, in_l = nxt_r, nxt_l

    slots = jnp.arange(n_row, dtype=jnp.int32)[None, :, None]
    out = jnp.zeros((sample_rows.shape[0], n_row, width), jnp.float32)
    for value, slot in tiles[:-1]:
        out = jnp.where(slots == slot, value[:, None, :], out)
    value, slot = tiles[-1]
    out = lax.optimization_barrier(out)
    return jnp.where(slots == slot, value[:, None, :], out)


def on_device(sample_frames, reference_frames, gain, flat, qbin, region, live):
    n_pix = lax.axis_size("pix")
    n_local = gain.shape[0]
    factor = gain / flat
    select = _bins(qbin)
    ref_select = select * (live * (1 - region)).astype(jnp.float32)[None, :]
    sample_mask = live * region
    sample_weight = sample_mask.astype(jnp.float32)
    full = (sample_frames, reference_frames, factor, ref_select, n_local * n_pix)

    n_chunk = 4 if n_local % 8 == 0 else 1
    chunk = n_local // n_chunk
    slots = chunk // 2
    keep = (sample_mask > 0).reshape(n_chunk, chunk)
    count = jnp.sum(keep.astype(jnp.int32), axis=1)
    if n_pix == 2:
        widest = jnp.max(jnp.maximum(count, _swap(count, "pix")))
    else:
        widest = lax.pmax(jnp.max(count), "pix")

    order = jnp.cumsum(keep.astype(jnp.int32), axis=1) - 1
    picks = keep[:, :, None] & (order[:, :, None] == jnp.arange(slots, dtype=jnp.int32)[None, None, :])
    picks = picks.astype(jnp.bfloat16)

    def cut(frames, picks=picks):
        pieces = [
            jnp.dot(frames[:, i * chunk:(i + 1) * chunk], picks[i], preferred_element_type=jnp.float32)
            for i in range(n_chunk)
        ]
        return jnp.concatenate(pieces, axis=1).astype(frames.dtype)

    table = jnp.stack([factor, qbin.astype(jnp.float32)])
    table = jnp.concatenate(
        [jnp.dot(table[:, i * chunk:(i + 1) * chunk], picks[i].astype(jnp.float32),
                 precision=lax.Precision.HIGHEST) for i in range(n_chunk)],
        axis=1,
    )
    used = (jnp.arange(slots, dtype=jnp.int32)[None, :] < count[:, None]).astype(jnp.float32)
    cut_operands = (picks, cut(reference_frames), table, used.reshape(-1))

    def compact(operands):
        picks, cut_reference, table, used = operands[2]
        return pipeline(cut(operands[0], picks), cut_reference, table[0], table[1].astype(jnp.int32), used, full)

    def whole(operands):
        sample_frames, reference_frames, _ = operands
        return pipeline(sample_frames, reference_frames, factor, qbin, sample_weight, full)

    out = lax.cond(widest <= slots, compact, whole, (sample_frames, reference_frames, cut_operands))
    return out[:, :, None, :]


def solution(mesh):
    return jax.shard_map(
        on_device,
        mesh=mesh,
        in_specs=(
            P(("row", "col"), "pix"),
            P(("row", "col"), "pix"),
            P("pix"),
            P("pix"),
            P("pix"),
            P("pix"),
            P("pix"),
        ),
        out_specs=P("row", None, "col", "pix"),
        check_vma=False,
    )
```

```python
import math

import jax
import jax.numpy as jnp
from jax import lax
from jax.sharding import PartitionSpec as P

QBINS = 32


def _swap(x, axis):
    return lax.ppermute(x, axis, [(0, 1), (1, 0)])


def _right(s, n):
    return [(i, i + 1) for i in range(s - 1, n - 1)]


def _left(s, n):
    return [(i, i - 1) for i in range(1, n - s + 1)]


def _bins(qbin):
    return (qbin[None, :] == jnp.arange(QBINS, dtype=jnp.int32)[:, None]).astype(jnp.float32)


def pipeline(raw_sample, raw_reference, factor_px, qbin_px, weight_px, full):
    sample_frames, reference_frames, factor, ref_select, n_total = full
    block = sample_frames.shape[0]
    n_row = lax.axis_size("row")
    n_pix = lax.axis_size("pix")
    r = lax.axis_index("row")
    p = lax.axis_index("pix")

    raw_rows = lax.all_gather(raw_sample, "col", axis=0, tiled=True)
    in_r = lax.ppermute(raw_reference, "row", _right(1, n_row))
    in_l = lax.ppermute(raw_reference, "row", _left(1, n_row))

    corrected_sample = sample_frames.astype(jnp.float32) * factor
    corrected_reference = reference_frames.astype(jnp.float32) * factor
    sums_sample = jnp.dot(corrected_sample, ref_select.T, precision=lax.Precision.HIGHEST)
    sums_reference = jnp.dot(corrected_reference, ref_select.T, precision=lax.Precision.HIGHEST)
    counts = jnp.sum(ref_select, axis=1)
    stats = (sums_sample, sums_reference, counts)
    if n_pix == 2:
        other = _swap(stats, "pix")
        stats = jax.tree.map(jnp.add, stats, other)
    else:
        stats = lax.psum(stats, "pix")
    sums_sample, sums_reference, counts = stats
    mean_sample = (sums_sample + 1.0) / (counts + 1.0)
    mean_reference = (sums_reference + 1.0) / (counts + 1.0)

    select = _bins(qbin_px)
    rows_mean = lax.all_gather(mean_sample, "col", axis=0, tiled=True)
    spread_rows = jnp.dot(rows_mean, select, precision=lax.Precision.HIGHEST)
    corrected_rows = raw_rows.astype(jnp.float32) * factor_px
    sample_rows = ((corrected_rows / spread_rows - 1.0) * weight_px).astype(jnp.bfloat16)

    def reference_deviation(frames, mean):
        spread = jnp.dot(mean, select, precision=lax.Precision.HIGHEST)
        return (frames.astype(jnp.float32) * factor_px / spread - 1.0).astype(jnp.bfloat16)

    scale = 1.0 / math.sqrt(n_total)
    width = block // n_pix

    def tile(frames, mean):
        part = lax.dot_general(
            sample_rows,
            reference_deviation(frames, mean),
            (((1,), (1,)), ((), ())),
            preferred_element_type=jnp.float32,
        )
        part = part * scale
        if n_pix == 2:
            keep = lax.dynamic_slice_in_dim(part, p * width, width, 1)
            give = lax.dynamic_slice_in_dim(part, (1 - p) * width, width, 1)
            return keep + _swap(give, "pix")
        return lax.psum_scatter(part, "pix", scatter_dimension=1, tiled=True)

    tiles = [(tile(raw_reference, mean_reference), r)]
    for s in range(1, n_row):
        if s + 1 < n_row:
            gate = [t for t, _ in tiles] if s > 1 else []
            fwd_r, fwd_l, _ = lax.optimization_barrier((in_r, in_l, gate))
            nxt_r = lax.ppermute(fwd_r, "row", _right(s + 1, n_row))
            nxt_l = lax.ppermute(fwd_l, "row", _left(s + 1, n_row))
        mean_r = lax.ppermute(mean_reference, "row", [(i, i + s) for i in range(n_row - s)])
        mean_l = lax.ppermute(mean_reference, "row", [(i, i - s) for i in range(s, n_row)])
        has_r = r >= s
        has_l = r + s < n_row
        if 2 * s < n_row:
            tiles.append((tile(in_r, mean_r), jnp.where(has_r, r - s, -1)))
            tiles.append((tile(in_l, mean_l), jnp.where(has_l, r + s, -1)))
        else:
            frames = jnp.where(has_r, in_r, in_l)
            mean = jnp.where(has_r, mean_r, mean_l)
            slot = jnp.where(has_r, r - s, jnp.where(has_l, r + s, -1))
            tiles.append((tile(frames, mean), slot))
        if s + 1 < n_row:
            in_r, in_l = nxt_r, nxt_l

    slots = jnp.arange(n_row, dtype=jnp.int32)[None, :, None]
    out = jnp.zeros((sample_rows.shape[0], n_row, width), jnp.float32)
    for value, slot in tiles[:-1]:
        out = jnp.where(slots == slot, value[:, None, :], out)
    value, slot = tiles[-1]
    out = lax.optimization_barrier(out)
    return jnp.where(slots == slot, value[:, None, :], out)


def on_device(sample_frames, reference_frames, gain, flat, qbin, region, live):
    n_pix = lax.axis_size("pix")
    n_local = gain.shape[0]
    factor = gain / flat
    select = _bins(qbin)
    ref_select = select * (live * (1 - region)).astype(jnp.float32)[None, :]
    sample_mask = live * region
    sample_weight = sample_mask.astype(jnp.float32)
    full = (sample_frames, reference_frames, factor, ref_select, n_local * n_pix)

    n_chunk = 4 if n_local % 8 == 0 else 1
    chunk = n_local // n_chunk
    slots = chunk // 2
    keep = (sample_mask > 0).reshape(n_chunk, chunk)
    count = jnp.sum(keep.astype(jnp.int32), axis=1)
    if n_pix == 2:
        widest = jnp.max(jnp.maximum(count, _swap(count, "pix")))
    else:
        widest = lax.pmax(jnp.max(count), "pix")

    order = jnp.cumsum(keep.astype(jnp.int32), axis=1) - 1
    picks = keep[:, :, None] & (order[:, :, None] == jnp.arange(slots, dtype=jnp.int32)[None, None, :])
    picks = picks.astype(jnp.bfloat16)

    def cut(frames):
        grouped = frames.reshape(frames.shape[0], n_chunk, chunk)
        kept = jnp.einsum("fck,cks->fcs", grouped, picks, preferred_element_type=jnp.float32)
        return kept.reshape(frames.shape[0], n_chunk * slots).astype(frames.dtype)

    table = jnp.stack([factor, qbin.astype(jnp.float32)])
    table = jnp.concatenate(
        [jnp.dot(table[:, i * chunk:(i + 1) * chunk], picks[i].astype(jnp.float32),
                 precision=lax.Precision.HIGHEST) for i in range(n_chunk)],
        axis=1,
    )
    used = (jnp.arange(slots, dtype=jnp.int32)[None, :] < count[:, None]).astype(jnp.float32)
    cut_operands = (cut(sample_frames), cut(reference_frames), table, used.reshape(-1))

    def compact(operands):
        cut_sample, cut_reference, table, used = operands[2]
        return pipeline(cut_sample, cut_reference, table[0], table[1].astype(jnp.int32), used, full)

    def whole(operands):
        sample_frames, reference_frames, _ = operands
        return pipeline(sample_frames, reference_frames, factor, qbin, sample_weight, full)

    out = lax.cond(widest <= slots, compact, whole, (sample_frames, reference_frames, cut_operands))
    return out[:, :, None, :]


def solution(mesh):
    return jax.shard_map(
        on_device,
        mesh=mesh,
        in_specs=(
            P(("row", "col"), "pix"),
            P(("row", "col"), "pix"),
            P("pix"),
            P("pix"),
            P("pix"),
            P("pix"),
            P("pix"),
        ),
        out_specs=P("row", None, "col", "pix"),
        check_vma=False,
    )
```

```python
import math

import jax
import jax.numpy as jnp
from jax import lax
from jax.sharding import PartitionSpec as P

QBINS = 32


def _swap(x, axis):
    return lax.ppermute(x, axis, [(0, 1), (1, 0)])


def _right(s, n):
    return [(i, i + 1) for i in range(s - 1, n - 1)]


def _left(s, n):
    return [(i, i - 1) for i in range(1, n - s + 1)]


def _bins(qbin):
    return (qbin[None, :] == jnp.arange(QBINS, dtype=jnp.int32)[:, None]).astype(jnp.float32)


def pipeline(raw_sample, raw_reference, factor_px, qbin_px, weight_px, full):
    sample_frames, reference_frames, factor, ref_select, n_total = full
    block = sample_frames.shape[0]
    n_row = lax.axis_size("row")
    n_pix = lax.axis_size("pix")
    r = lax.axis_index("row")
    p = lax.axis_index("pix")

    raw_rows = lax.all_gather(raw_sample, "col", axis=0, tiled=True)
    in_r = lax.ppermute(raw_reference, "row", _right(1, n_row))
    in_l = lax.ppermute(raw_reference, "row", _left(1, n_row))

    corrected_sample = sample_frames.astype(jnp.float32) * factor
    corrected_reference = reference_frames.astype(jnp.float32) * factor
    sums_sample = jnp.dot(corrected_sample, ref_select.T, precision=lax.Precision.HIGHEST)
    sums_reference = jnp.dot(corrected_reference, ref_select.T, precision=lax.Precision.HIGHEST)
    counts = jnp.sum(ref_select, axis=1)
    stats = (sums_sample, sums_reference, counts)
    if n_pix == 2:
        other = _swap(stats, "pix")
        stats = jax.tree.map(jnp.add, stats, other)
    else:
        stats = lax.psum(stats, "pix")
    sums_sample, sums_reference, counts = stats
    mean_sample = (sums_sample + 1.0) / (counts + 1.0)
    mean_reference = (sums_reference + 1.0) / (counts + 1.0)

    select = _bins(qbin_px)
    rows_mean = lax.all_gather(mean_sample, "col", axis=0, tiled=True)
    spread_rows = jnp.dot(rows_mean, select, precision=lax.Precision.HIGHEST)
    corrected_rows = raw_rows.astype(jnp.float32) * factor_px
    sample_rows = ((corrected_rows / spread_rows - 1.0) * weight_px).astype(jnp.bfloat16)

    def reference_deviation(frames, mean):
        spread = jnp.dot(mean, select, precision=lax.Precision.HIGHEST)
        return (frames.astype(jnp.float32) * factor_px / spread - 1.0).astype(jnp.bfloat16)

    scale = 1.0 / math.sqrt(n_total)
    width = block // n_pix

    def tile(frames, mean):
        part = lax.dot_general(
            sample_rows,
            reference_deviation(frames, mean),
            (((1,), (1,)), ((), ())),
            preferred_element_type=jnp.float32,
        )
        part = part * scale
        if n_pix == 2:
            keep = lax.dynamic_slice_in_dim(part, p * width, width, 1)
            give = lax.dynamic_slice_in_dim(part, (1 - p) * width, width, 1)
            return keep + _swap(give, "pix")
        return lax.psum_scatter(part, "pix", scatter_dimension=1, tiled=True)

    tiles = [(tile(raw_reference, mean_reference), r)]
    for s in range(1, n_row):
        if s + 1 < n_row:
            gate = [t for t, _ in tiles] if s > 1 else []
            fwd_r, fwd_l, _ = lax.optimization_barrier((in_r, in_l, gate))
            nxt_r = lax.ppermute(fwd_r, "row", _right(s + 1, n_row))
            nxt_l = lax.ppermute(fwd_l, "row", _left(s + 1, n_row))
        mean_r = lax.ppermute(mean_reference, "row", [(i, i + s) for i in range(n_row - s)])
        mean_l = lax.ppermute(mean_reference, "row", [(i, i - s) for i in range(s, n_row)])
        has_r = r >= s
        has_l = r + s < n_row
        if 2 * s < n_row:
            tiles.append((tile(in_r, mean_r), jnp.where(has_r, r - s, -1)))
            tiles.append((tile(in_l, mean_l), jnp.where(has_l, r + s, -1)))
        else:
            frames = jnp.where(has_r, in_r, in_l)
            mean = jnp.where(has_r, mean_r, mean_l)
            slot = jnp.where(has_r, r - s, jnp.where(has_l, r + s, -1))
            tiles.append((tile(frames, mean), slot))
        if s + 1 < n_row:
            in_r, in_l = nxt_r, nxt_l

    slots = jnp.arange(n_row, dtype=jnp.int32)[None, :, None]
    out = jnp.zeros((sample_rows.shape[0], n_row, width), jnp.float32)
    for value, slot in tiles[:-1]:
        out = jnp.where(slots == slot, value[:, None, :], out)
    value, slot = tiles[-1]
    out = lax.optimization_barrier(out)
    return jnp.where(slots == slot, value[:, None, :], out)


def on_device(sample_frames, reference_frames, gain, flat, qbin, region, live):
    n_pix = lax.axis_size("pix")
    n_local = gain.shape[0]
    factor = gain / flat
    select = _bins(qbin)
    ref_select = select * (live * (1 - region)).astype(jnp.float32)[None, :]
    sample_mask = live * region
    sample_weight = sample_mask.astype(jnp.float32)
    full = (sample_frames, reference_frames, factor, ref_select, n_local * n_pix)

    n_chunk = 4 if n_local % 8 == 0 else 1
    chunk = n_local // n_chunk
    slots = chunk // 2
    keep = (sample_mask > 0).reshape(n_chunk, chunk)
    count = jnp.sum(keep.astype(jnp.int32), axis=1)
    if n_pix == 2:
        widest = jnp.max(jnp.maximum(count, _swap(count, "pix")))
    else:
        widest = lax.pmax(jnp.max(count), "pix")

    order = jnp.cumsum(keep.astype(jnp.int32), axis=1) - 1
    picks = keep[:, :, None] & (order[:, :, None] == jnp.arange(slots, dtype=jnp.int32)[None, None, :])
    picks = picks.astype(jnp.bfloat16)

    def cut(frames):
        pieces = [
            jnp.dot(frames[:, i * chunk:(i + 1) * chunk], picks[i], preferred_element_type=jnp.float32)
            for i in range(n_chunk)
        ]
        return jnp.concatenate(pieces, axis=1).astype(frames.dtype)

    table = jnp.stack([factor, qbin.astype(jnp.float32)])
    table = jnp.concatenate(
        [jnp.dot(table[:, i * chunk:(i + 1) * chunk], picks[i].astype(jnp.float32),
                 precision=lax.Precision.HIGH) for i in range(n_chunk)],
        axis=1,
    )
    used = (jnp.arange(slots, dtype=jnp.int32)[None, :] < count[:, None]).astype(jnp.float32)
    cut_operands = (cut(sample_frames), cut(reference_frames), table, used.reshape(-1))

    def compact(operands):
        cut_sample, cut_reference, table, used = operands[2]
        return pipeline(cut_sample, cut_reference, table[0], table[1].astype(jnp.int32), used, full)

    def whole(operands):
        sample_frames, reference_frames, _ = operands
        return pipeline(sample_frames, reference_frames, factor, qbin, sample_weight, full)

    out = lax.cond(widest <= slots, compact, whole, (sample_frames, reference_frames, cut_operands))
    return out[:, :, None, :]


def solution(mesh):
    return jax.shard_map(
        on_device,
        mesh=mesh,
        in_specs=(
            P(("row", "col"), "pix"),
            P(("row", "col"), "pix"),
            P("pix"),
            P("pix"),
            P("pix"),
            P("pix"),
            P("pix"),
        ),
        out_specs=P("row", None, "col", "pix"),
        check_vma=False,
    )
```

```python
import math

import jax
import jax.numpy as jnp
from jax import lax
from jax.sharding import PartitionSpec as P

QBINS = 32


def _swap(x, axis):
    return lax.ppermute(x, axis, [(0, 1), (1, 0)])


def _right(s, n):
    return [(i, i + 1) for i in range(s - 1, n - 1)]


def _left(s, n):
    return [(i, i - 1) for i in range(1, n - s + 1)]


def _bins(qbin):
    return (qbin[None, :] == jnp.arange(QBINS, dtype=jnp.int32)[:, None]).astype(jnp.float32)


def pipeline(raw_sample, raw_reference, factor_px, qbin_px, weight_px, full):
    sample_frames, reference_frames, factor, ref_select, n_total = full
    block = sample_frames.shape[0]
    n_row = lax.axis_size("row")
    n_pix = lax.axis_size("pix")
    r = lax.axis_index("row")
    p = lax.axis_index("pix")

    raw_rows = lax.all_gather(raw_sample, "col", axis=0, tiled=True)
    in_r = lax.ppermute(raw_reference, "row", _right(1, n_row))
    in_l = lax.ppermute(raw_reference, "row", _left(1, n_row))

    corrected_sample = sample_frames.astype(jnp.float32) * factor
    corrected_reference = reference_frames.astype(jnp.float32) * factor
    sums_sample = jnp.dot(corrected_sample, ref_select.T, precision=lax.Precision.HIGHEST)
    sums_reference = jnp.dot(corrected_reference, ref_select.T, precision=lax.Precision.HIGHEST)
    counts = jnp.sum(ref_select, axis=1)
    stats = (sums_sample, sums_reference, counts)
    if n_pix == 2:
        other = _swap(stats, "pix")
        stats = jax.tree.map(jnp.add, stats, other)
    else:
        stats = lax.psum(stats, "pix")
    sums_sample, sums_reference, counts = stats
    mean_sample = (sums_sample + 1.0) / (counts + 1.0)
    mean_reference = (sums_reference + 1.0) / (counts + 1.0)

    select = _bins(qbin_px)
    rows_mean = lax.all_gather(mean_sample, "col", axis=0, tiled=True)
    spread_rows = jnp.dot(rows_mean, select, precision=lax.Precision.HIGHEST)
    corrected_rows = raw_rows.astype(jnp.float32) * factor_px
    sample_rows = ((corrected_rows / spread_rows - 1.0) * weight_px).astype(jnp.bfloat16)

    def reference_deviation(frames, mean):
        spread = jnp.dot(mean, select, precision=lax.Precision.HIGHEST)
        return (frames.astype(jnp.float32) * factor_px / spread - 1.0).astype(jnp.bfloat16)

    scale = 1.0 / math.sqrt(n_total)
    width = block // n_pix

    def tile(frames, mean, pieces=1):
        deviation = reference_deviation(frames, mean)
        step = sample_rows.shape[0] // pieces
        done = []
        for j in range(pieces):
            part = lax.dot_general(
                sample_rows[j * step:(j + 1) * step],
                deviation,
                (((1,), (1,)), ((), ())),
                preferred_element_type=jnp.float32,
            )
            part = part * scale
            if n_pix == 2:
                keep = lax.dynamic_slice_in_dim(part, p * width, width, 1)
                give = lax.dynamic_slice_in_dim(part, (1 - p) * width, width, 1)
                done.append(keep + _swap(give, "pix"))
            else:
                done.append(lax.psum_scatter(part, "pix", scatter_dimension=1, tiled=True))
        return done[0] if pieces == 1 else jnp.concatenate(done, axis=0)

    tiles = [(tile(raw_reference, mean_reference), r)]
    for s in range(1, n_row):
        if s + 1 < n_row:
            gate = [t for t, _ in tiles] if s > 1 else []
            fwd_r, fwd_l, _ = lax.optimization_barrier((in_r, in_l, gate))
            nxt_r = lax.ppermute(fwd_r, "row", _right(s + 1, n_row))
            nxt_l = lax.ppermute(fwd_l, "row", _left(s + 1, n_row))
        mean_r = lax.ppermute(mean_reference, "row", [(i, i + s) for i in range(n_row - s)])
        mean_l = lax.ppermute(mean_reference, "row", [(i, i - s) for i in range(s, n_row)])
        has_r = r >= s
        has_l = r + s < n_row
        if 2 * s < n_row:
            tiles.append((tile(in_r, mean_r), jnp.where(has_r, r - s, -1)))
            tiles.append((tile(in_l, mean_l), jnp.where(has_l, r + s, -1)))
        else:
            frames = jnp.where(has_r, in_r, in_l)
            mean = jnp.where(has_r, mean_r, mean_l)
            slot = jnp.where(has_r, r - s, jnp.where(has_l, r + s, -1))
            tiles.append((tile(frames, mean, 2 if s + 1 == n_row else 1), slot))
        if s + 1 < n_row:
            in_r, in_l = nxt_r, nxt_l

    slots = jnp.arange(n_row, dtype=jnp.int32)[None, :, None]
    out = jnp.zeros((sample_rows.shape[0], n_row, width), jnp.float32)
    for value, slot in tiles[:-1]:
        out = jnp.where(slots == slot, value[:, None, :], out)
    value, slot = tiles[-1]
    out = lax.optimization_barrier(out)
    return jnp.where(slots == slot, value[:, None, :], out)


def on_device(sample_frames, reference_frames, gain, flat, qbin, region, live):
    n_pix = lax.axis_size("pix")
    n_local = gain.shape[0]
    factor = gain / flat
    select = _bins(qbin)
    ref_select = select * (live * (1 - region)).astype(jnp.float32)[None, :]
    sample_mask = live * region
    sample_weight = sample_mask.astype(jnp.float32)
    full = (sample_frames, reference_frames, factor, ref_select, n_local * n_pix)

    n_chunk = 4 if n_local % 8 == 0 else 1
    chunk = n_local // n_chunk
    slots = chunk // 2
    keep = (sample_mask > 0).reshape(n_chunk, chunk)
    count = jnp.sum(keep.astype(jnp.int32), axis=1)
    if n_pix == 2:
        widest = jnp.max(jnp.maximum(count, _swap(count, "pix")))
    else:
        widest = lax.pmax(jnp.max(count), "pix")

    order = jnp.cumsum(keep.astype(jnp.int32), axis=1) - 1
    picks = keep[:, :, None] & (order[:, :, None] == jnp.arange(slots, dtype=jnp.int32)[None, None, :])
    picks = picks.astype(jnp.bfloat16)

    def cut(frames):
        pieces = [
            jnp.dot(frames[:, i * chunk:(i + 1) * chunk], picks[i], preferred_element_type=jnp.float32)
            for i in range(n_chunk)
        ]
        return jnp.concatenate(pieces, axis=1).astype(frames.dtype)

    table = jnp.stack([factor, qbin.astype(jnp.float32)])
    table = jnp.concatenate(
        [jnp.dot(table[:, i * chunk:(i + 1) * chunk], picks[i].astype(jnp.float32),
                 precision=lax.Precision.HIGH) for i in range(n_chunk)],
        axis=1,
    )
    used = (jnp.arange(slots, dtype=jnp.int32)[None, :] < count[:, None]).astype(jnp.float32)
    cut_operands = (cut(sample_frames), cut(reference_frames), table, used.reshape(-1))

    def compact(operands):
        cut_sample, cut_reference, table, used = operands[2]
        return pipeline(cut_sample, cut_reference, table[0], table[1].astype(jnp.int32), used, full)

    def whole(operands):
        sample_frames, reference_frames, _ = operands
        return pipeline(sample_frames, reference_frames, factor, qbin, sample_weight, full)

    out = lax.cond(widest <= slots, compact, whole, (sample_frames, reference_frames, cut_operands))
    return out[:, :, None, :]


def solution(mesh):
    return jax.shard_map(
        on_device,
        mesh=mesh,
        in_specs=(
            P(("row", "col"), "pix"),
            P(("row", "col"), "pix"),
            P("pix"),
            P("pix"),
            P("pix"),
            P("pix"),
            P("pix"),
        ),
        out_specs=P("row", None, "col", "pix"),
        check_vma=False,
    )
```

```python
import math

import jax
import jax.numpy as jnp
from jax import lax
from jax.sharding import PartitionSpec as P

QBINS = 32


def _swap(x, axis):
    return lax.ppermute(x, axis, [(0, 1), (1, 0)])


def _right(s, n):
    return [(i, i + 1) for i in range(s - 1, n - 1)]


def _left(s, n):
    return [(i, i - 1) for i in range(1, n - s + 1)]


def _bins(qbin):
    return (qbin[None, :] == jnp.arange(QBINS, dtype=jnp.int32)[:, None]).astype(jnp.float32)


def pipeline(raw_sample, raw_reference, factor_px, qbin_px, weight_px, full):
    sample_frames, reference_frames, factor, ref_select, n_total = full
    block = sample_frames.shape[0]
    n_row = lax.axis_size("row")
    n_pix = lax.axis_size("pix")
    r = lax.axis_index("row")
    p = lax.axis_index("pix")

    raw_rows = lax.all_gather(raw_sample, "col", axis=0, tiled=True)
    in_r = lax.ppermute(raw_reference, "row", _right(1, n_row))
    in_l = lax.ppermute(raw_reference, "row", _left(1, n_row))

    corrected_sample = sample_frames.astype(jnp.float32) * factor
    corrected_reference = reference_frames.astype(jnp.float32) * factor
    sums_sample = jnp.dot(corrected_sample, ref_select.T, precision=lax.Precision.HIGHEST)
    sums_reference = jnp.dot(corrected_reference, ref_select.T, precision=lax.Precision.HIGHEST)
    counts = jnp.sum(ref_select, axis=1)
    stats = (sums_sample, sums_reference, counts)
    if n_pix == 2:
        other = _swap(stats, "pix")
        stats = jax.tree.map(jnp.add, stats, other)
    else:
        stats = lax.psum(stats, "pix")
    sums_sample, sums_reference, counts = stats
    mean_sample = (sums_sample + 1.0) / (counts + 1.0)
    mean_reference = (sums_reference + 1.0) / (counts + 1.0)

    select = _bins(qbin_px)
    rows_mean = lax.all_gather(mean_sample, "col", axis=0, tiled=True)
    spread_rows = jnp.dot(rows_mean, select, precision=lax.Precision.HIGHEST)
    corrected_rows = raw_rows.astype(jnp.float32) * factor_px
    sample_rows = ((corrected_rows / spread_rows - 1.0) * weight_px).astype(jnp.bfloat16)

    def reference_deviation(frames, mean):
        spread = jnp.dot(mean, select, precision=lax.Precision.HIGHEST)
        return (frames.astype(jnp.float32) * factor_px / spread - 1.0).astype(jnp.bfloat16)

    scale = 1.0 / math.sqrt(n_total)
    width = block // n_pix

    def tile(frames, mean):
        part = lax.dot_general(
            sample_rows,
            reference_deviation(frames, mean),
            (((1,), (1,)), ((), ())),
            preferred_element_type=jnp.float32,
        )
        part = part * scale
        if n_pix == 2:
            keep = lax.dynamic_slice_in_dim(part, p * width, width, 1)
            give = lax.dynamic_slice_in_dim(part, (1 - p) * width, width, 1)
            return keep + _swap(give, "pix")
        return lax.psum_scatter(part, "pix", scatter_dimension=1, tiled=True)

    tiles = [(tile(raw_reference, mean_reference), r)]
    for s in range(1, n_row):
        if s + 1 < n_row:
            gate = [t for t, _ in tiles] if s > 1 else []
            fwd_r, fwd_l, _ = lax.optimization_barrier((in_r, in_l, gate))
            nxt_r = lax.ppermute(fwd_r, "row", _right(s + 1, n_row))
            nxt_l = lax.ppermute(fwd_l, "row", _left(s + 1, n_row))
        mean_r = lax.ppermute(mean_reference, "row", [(i, i + s) for i in range(n_row - s)])
        mean_l = lax.ppermute(mean_reference, "row", [(i, i - s) for i in range(s, n_row)])
        has_r = r >= s
        has_l = r + s < n_row
        if 2 * s < n_row:
            tiles.append((tile(in_r, mean_r), jnp.where(has_r, r - s, -1)))
            tiles.append((tile(in_l, mean_l), jnp.where(has_l, r + s, -1)))
        else:
            frames = jnp.where(has_r, in_r, in_l)
            mean = jnp.where(has_r, mean_r, mean_l)
            slot = jnp.where(has_r, r - s, jnp.where(has_l, r + s, -1))
            tiles.append((tile(frames, mean), slot))
        if s + 1 < n_row:
            in_r, in_l = nxt_r, nxt_l

    slots = jnp.arange(n_row, dtype=jnp.int32)[None, :, None]
    out = jnp.zeros((sample_rows.shape[0], n_row, width), jnp.float32)
    for value, slot in tiles[:-1]:
        out = jnp.where(slots == slot, value[:, None, :], out)
    value, slot = tiles[-1]
    out = lax.optimization_barrier(out)
    return jnp.where(slots == slot, value[:, None, :], out)


def on_device(sample_frames, reference_frames, gain, flat, qbin, region, live):
    n_pix = lax.axis_size("pix")
    n_local = gain.shape[0]
    factor = gain / flat
    select = _bins(qbin)
    ref_select = select * (live * (1 - region)).astype(jnp.float32)[None, :]
    sample_mask = live * region
    sample_weight = sample_mask.astype(jnp.float32)
    full = (sample_frames, reference_frames, factor, ref_select, n_local * n_pix)

    n_chunk = 4 if n_local % 8 == 0 else 1
    chunk = n_local // n_chunk
    slots = chunk // 2
    keep = (sample_mask > 0).reshape(n_chunk, chunk)
    count = jnp.sum(keep.astype(jnp.int32), axis=1)
    if n_pix == 2:
        widest = jnp.max(jnp.maximum(count, _swap(count, "pix")))
    else:
        widest = lax.pmax(jnp.max(count), "pix")

    order = jnp.cumsum(keep.astype(jnp.int32), axis=1) - 1
    picks = keep[:, :, None] & (order[:, :, None] == jnp.arange(slots, dtype=jnp.int32)[None, None, :])
    picks = picks.astype(jnp.bfloat16)

    def cut(frames):
        pieces = [
            jnp.dot(frames[:, i * chunk:(i + 1) * chunk], picks[i], preferred_element_type=jnp.float32)
            for i in range(n_chunk)
        ]
        return jnp.concatenate(pieces, axis=1).astype(frames.dtype)

    hi = lax.reduce_precision(factor, exponent_bits=8, mantissa_bits=7)
    mid = lax.reduce_precision(factor - hi, exponent_bits=8, mantissa_bits=7)
    lo = factor - hi - mid
    table = jnp.stack([hi, mid, lo, qbin.astype(jnp.float32)]).astype(jnp.bfloat16)
    table = jnp.concatenate(
        [jnp.dot(table[:, i * chunk:(i + 1) * chunk], picks[i], preferred_element_type=jnp.float32)
         for i in range(n_chunk)],
        axis=1,
    )
    table = jnp.stack([(table[0] + table[1]) + table[2], table[3]])
    used = (jnp.arange(slots, dtype=jnp.int32)[None, :] < count[:, None]).astype(jnp.float32)
    cut_operands = (cut(sample_frames), cut(reference_frames), table, used.reshape(-1))

    def compact(operands):
        cut_sample, cut_reference, table, used = operands[2]
        return pipeline(cut_sample, cut_reference, table[0], table[1].astype(jnp.int32), used, full)

    def whole(operands):
        sample_frames, reference_frames, _ = operands
        return pipeline(sample_frames, reference_frames, factor, qbin, sample_weight, full)

    out = lax.cond(widest <= slots, compact, whole, (sample_frames, reference_frames, cut_operands))
    return out[:, :, None, :]


def solution(mesh):
    return jax.shard_map(
        on_device,
        mesh=mesh,
        in_specs=(
            P(("row", "col"), "pix"),
            P(("row", "col"), "pix"),
            P("pix"),
            P("pix"),
            P("pix"),
            P("pix"),
            P("pix"),
        ),
        out_specs=P("row", None, "col", "pix"),
        check_vma=False,
    )
```

```python
import math

import jax
import jax.numpy as jnp
from jax import lax
from jax.sharding import PartitionSpec as P

QBINS = 32


def _swap(x, axis):
    return lax.ppermute(x, axis, [(0, 1), (1, 0)])


def _right(s, n):
    return [(i, i + 1) for i in range(s - 1, n - 1)]


def _left(s, n):
    return [(i, i - 1) for i in range(1, n - s + 1)]


def _bins(qbin):
    return (qbin[None, :] == jnp.arange(QBINS, dtype=jnp.int32)[:, None]).astype(jnp.float32)


def pipeline(raw_sample, raw_reference, factor_px, qbin_px, weight_px, full):
    sample_frames, reference_frames, factor, ref_select, n_total = full
    block = sample_frames.shape[0]
    n_row = lax.axis_size("row")
    n_pix = lax.axis_size("pix")
    r = lax.axis_index("row")
    p = lax.axis_index("pix")

    raw_rows = lax.all_gather(raw_sample, "col", axis=0, tiled=True)
    in_r = lax.ppermute(raw_reference, "row", _right(1, n_row))
    in_l = lax.ppermute(raw_reference, "row", _left(1, n_row))

    corrected_sample = sample_frames.astype(jnp.float32) * factor
    corrected_reference = reference_frames.astype(jnp.float32) * factor
    sums_sample = jnp.dot(corrected_sample, ref_select.T, precision=lax.Precision.HIGHEST)
    sums_reference = jnp.dot(corrected_reference, ref_select.T, precision=lax.Precision.HIGHEST)
    counts = jnp.sum(ref_select, axis=1)
    stats = (sums_sample, sums_reference, counts)
    if n_pix == 2:
        other = _swap(stats, "pix")
        stats = jax.tree.map(jnp.add, stats, other)
    else:
        stats = lax.psum(stats, "pix")
    sums_sample, sums_reference, counts = stats
    mean_sample = (sums_sample + 1.0) / (counts + 1.0)
    mean_reference = (sums_reference + 1.0) / (counts + 1.0)

    select = _bins(qbin_px)
    rows_mean = lax.all_gather(mean_sample, "col", axis=0, tiled=True)
    spread_rows = jnp.dot(rows_mean, select, precision=lax.Precision.HIGHEST)
    corrected_rows = raw_rows.astype(jnp.float32) * factor_px
    sample_rows = ((corrected_rows / spread_rows - 1.0) * weight_px).astype(jnp.bfloat16)

    def reference_deviation(frames, mean):
        spread = jnp.dot(select.T, mean.T, precision=lax.Precision.HIGHEST)
        return (frames.astype(jnp.float32) * factor_px[:, None] / spread - 1.0).astype(jnp.bfloat16)

    scale = 1.0 / math.sqrt(n_total)
    width = block // n_pix

    def tile(frames, mean):
        part = lax.dot_general(
            sample_rows,
            reference_deviation(frames, mean),
            (((1,), (0,)), ((), ())),
            preferred_element_type=jnp.float32,
        )
        part = part * scale
        if n_pix == 2:
            keep = lax.dynamic_slice_in_dim(part, p * width, width, 1)
            give = lax.dynamic_slice_in_dim(part, (1 - p) * width, width, 1)
            return keep + _swap(give, "pix")
        return lax.psum_scatter(part, "pix", scatter_dimension=1, tiled=True)

    tiles = [(tile(raw_reference, mean_reference), r)]
    for s in range(1, n_row):
        if s + 1 < n_row:
            gate = [t for t, _ in tiles] if s > 1 else []
            fwd_r, fwd_l, _ = lax.optimization_barrier((in_r, in_l, gate))
            nxt_r = lax.ppermute(fwd_r, "row", _right(s + 1, n_row))
            nxt_l = lax.ppermute(fwd_l, "row", _left(s + 1, n_row))
        mean_r = lax.ppermute(mean_reference, "row", [(i, i + s) for i in range(n_row - s)])
        mean_l = lax.ppermute(mean_reference, "row", [(i, i - s) for i in range(s, n_row)])
        has_r = r >= s
        has_l = r + s < n_row
        if 2 * s < n_row:
            tiles.append((tile(in_r, mean_r), jnp.where(has_r, r - s, -1)))
            tiles.append((tile(in_l, mean_l), jnp.where(has_l, r + s, -1)))
        else:
            frames = jnp.where(has_r, in_r, in_l)
            mean = jnp.where(has_r, mean_r, mean_l)
            slot = jnp.where(has_r, r - s, jnp.where(has_l, r + s, -1))
            tiles.append((tile(frames, mean), slot))
        if s + 1 < n_row:
            in_r, in_l = nxt_r, nxt_l

    slots = jnp.arange(n_row, dtype=jnp.int32)[None, :, None]
    out = jnp.zeros((sample_rows.shape[0], n_row, width), jnp.float32)
    for value, slot in tiles[:-1]:
        out = jnp.where(slots == slot, value[:, None, :], out)
    value, slot = tiles[-1]
    out = lax.optimization_barrier(out)
    return jnp.where(slots == slot, value[:, None, :], out)


def on_device(sample_frames, reference_frames, gain, flat, qbin, region, live):
    n_pix = lax.axis_size("pix")
    n_local = gain.shape[0]
    factor = gain / flat
    select = _bins(qbin)
    ref_select = select * (live * (1 - region)).astype(jnp.float32)[None, :]
    sample_mask = live * region
    sample_weight = sample_mask.astype(jnp.float32)
    full = (sample_frames, reference_frames, factor, ref_select, n_local * n_pix)

    n_chunk = 4 if n_local % 8 == 0 else 1
    chunk = n_local // n_chunk
    slots = chunk // 2
    keep = (sample_mask > 0).reshape(n_chunk, chunk)
    count = jnp.sum(keep.astype(jnp.int32), axis=1)
    if n_pix == 2:
        widest = jnp.max(jnp.maximum(count, _swap(count, "pix")))
    else:
        widest = lax.pmax(jnp.max(count), "pix")

    order = jnp.cumsum(keep.astype(jnp.int32), axis=1) - 1
    picks = keep[:, :, None] & (order[:, :, None] == jnp.arange(slots, dtype=jnp.int32)[None, None, :])
    picks = picks.astype(jnp.bfloat16)

    def cut(frames):
        pieces = [
            jnp.dot(frames[:, i * chunk:(i + 1) * chunk], picks[i], preferred_element_type=jnp.float32)
            for i in range(n_chunk)
        ]
        return jnp.concatenate(pieces, axis=1).astype(frames.dtype)

    hi = lax.reduce_precision(factor, exponent_bits=8, mantissa_bits=7)
    mid = lax.reduce_precision(factor - hi, exponent_bits=8, mantissa_bits=7)
    lo = factor - hi - mid
    table = jnp.stack([hi, mid, lo, qbin.astype(jnp.float32)]).astype(jnp.bfloat16)
    table = jnp.concatenate(
        [jnp.dot(table[:, i * chunk:(i + 1) * chunk], picks[i], preferred_element_type=jnp.float32)
         for i in range(n_chunk)],
        axis=1,
    )
    table = jnp.stack([(table[0] + table[1]) + table[2], table[3]])
    used = (jnp.arange(slots, dtype=jnp.int32)[None, :] < count[:, None]).astype(jnp.float32)
    cut_operands = (cut(sample_frames), cut(reference_frames).T, table, used.reshape(-1))

    def compact(operands):
        cut_sample, cut_reference, table, used = operands[2]
        return pipeline(cut_sample, cut_reference, table[0], table[1].astype(jnp.int32), used, full)

    def whole(operands):
        sample_frames, reference_frames, _ = operands
        return pipeline(sample_frames, reference_frames.T, factor, qbin, sample_weight, full)

    out = lax.cond(widest <= slots, compact, whole, (sample_frames, reference_frames, cut_operands))
    return out[:, :, None, :]


def solution(mesh):
    return jax.shard_map(
        on_device,
        mesh=mesh,
        in_specs=(
            P(("row", "col"), "pix"),
            P(("row", "col"), "pix"),
            P("pix"),
            P("pix"),
            P("pix"),
            P("pix"),
            P("pix"),
        ),
        out_specs=P("row", None, "col", "pix"),
        check_vma=False,
    )
```

```python
import math

import jax
import jax.numpy as jnp
from jax import lax
from jax.sharding import PartitionSpec as P

QBINS = 32


def _swap(x, axis):
    return lax.ppermute(x, axis, [(0, 1), (1, 0)])


def _right(s, n):
    return [(i, i + 1) for i in range(s - 1, n - 1)]


def _left(s, n):
    return [(i, i - 1) for i in range(1, n - s + 1)]


def _bins(qbin):
    return (qbin[None, :] == jnp.arange(QBINS, dtype=jnp.int32)[:, None]).astype(jnp.float32)


def pipeline(raw_sample, raw_reference, factor_px, qbin_px, weight_px, full):
    sample_frames, reference_frames, factor, ref_select, n_total = full
    block = sample_frames.shape[0]
    n_row = lax.axis_size("row")
    n_pix = lax.axis_size("pix")
    r = lax.axis_index("row")
    p = lax.axis_index("pix")

    raw_rows = lax.all_gather(raw_sample, "col", axis=1, tiled=True)
    in_r = lax.ppermute(raw_reference, "row", _right(1, n_row))
    in_l = lax.ppermute(raw_reference, "row", _left(1, n_row))

    corrected_sample = sample_frames.astype(jnp.float32) * factor
    corrected_reference = reference_frames.astype(jnp.float32) * factor
    sums_sample = jnp.dot(corrected_sample, ref_select.T, precision=lax.Precision.HIGHEST)
    sums_reference = jnp.dot(corrected_reference, ref_select.T, precision=lax.Precision.HIGHEST)
    counts = jnp.sum(ref_select, axis=1)
    stats = (sums_sample, sums_reference, counts)
    if n_pix == 2:
        other = _swap(stats, "pix")
        stats = jax.tree.map(jnp.add, stats, other)
    else:
        stats = lax.psum(stats, "pix")
    sums_sample, sums_reference, counts = stats
    mean_sample = (sums_sample + 1.0) / (counts + 1.0)
    mean_reference = (sums_reference + 1.0) / (counts + 1.0)

    select = _bins(qbin_px)
    rows_mean = lax.all_gather(mean_sample, "col", axis=0, tiled=True)
    spread_rows = jnp.dot(select.T, rows_mean.T, precision=lax.Precision.HIGHEST)
    corrected_rows = raw_rows.astype(jnp.float32) * factor_px[:, None]
    sample_rows = ((corrected_rows / spread_rows - 1.0) * weight_px[:, None]).astype(jnp.bfloat16)

    def reference_deviation(frames, mean):
        spread = jnp.dot(select.T, mean.T, precision=lax.Precision.HIGHEST)
        return (frames.astype(jnp.float32) * factor_px[:, None] / spread - 1.0).astype(jnp.bfloat16)

    scale = 1.0 / math.sqrt(n_total)
    width = block // n_pix

    def tile(frames, mean):
        part = lax.dot_general(
            sample_rows,
            reference_deviation(frames, mean),
            (((0,), (0,)), ((), ())),
            preferred_element_type=jnp.float32,
        )
        part = part * scale
        if n_pix == 2:
            keep = lax.dynamic_slice_in_dim(part, p * width, width, 1)
            give = lax.dynamic_slice_in_dim(part, (1 - p) * width, width, 1)
            return keep + _swap(give, "pix")
        return lax.psum_scatter(part, "pix", scatter_dimension=1, tiled=True)

    tiles = [(tile(raw_reference, mean_reference), r)]
    for s in range(1, n_row):
        if s + 1 < n_row:
            gate = [t for t, _ in tiles] if s > 1 else []
            fwd_r, fwd_l, _ = lax.optimization_barrier((in_r, in_l, gate))
            nxt_r = lax.ppermute(fwd_r, "row", _right(s + 1, n_row))
            nxt_l = lax.ppermute(fwd_l, "row", _left(s + 1, n_row))
        mean_r = lax.ppermute(mean_reference, "row", [(i, i + s) for i in range(n_row - s)])
        mean_l = lax.ppermute(mean_reference, "row", [(i, i - s) for i in range(s, n_row)])
        has_r = r >= s
        has_l = r + s < n_row
        if 2 * s < n_row:
            tiles.append((tile(in_r, mean_r), jnp.where(has_r, r - s, -1)))
            tiles.append((tile(in_l, mean_l), jnp.where(has_l, r + s, -1)))
        else:
            frames = jnp.where(has_r, in_r, in_l)
            mean = jnp.where(has_r, mean_r, mean_l)
            slot = jnp.where(has_r, r - s, jnp.where(has_l, r + s, -1))
            tiles.append((tile(frames, mean), slot))
        if s + 1 < n_row:
            in_r, in_l = nxt_r, nxt_l

    slots = jnp.arange(n_row, dtype=jnp.int32)[None, :, None]
    out = jnp.zeros((sample_rows.shape[1], n_row, width), jnp.float32)
    for value, slot in tiles[:-1]:
        out = jnp.where(slots == slot, value[:, None, :], out)
    value, slot = tiles[-1]
    out = lax.optimization_barrier(out)
    return jnp.where(slots == slot, value[:, None, :], out)


def on_device(sample_frames, reference_frames, gain, flat, qbin, region, live):
    n_pix = lax.axis_size("pix")
    n_local = gain.shape[0]
    factor = gain / flat
    select = _bins(qbin)
    ref_select = select * (live * (1 - region)).astype(jnp.float32)[None, :]
    sample_mask = live * region
    sample_weight = sample_mask.astype(jnp.float32)
    full = (sample_frames, reference_frames, factor, ref_select, n_local * n_pix)

    n_chunk = 4 if n_local % 8 == 0 else 1
    chunk = n_local // n_chunk
    slots = chunk // 2
    keep = (sample_mask > 0).reshape(n_chunk, chunk)
    count = jnp.sum(keep.astype(jnp.int32), axis=1)
    if n_pix == 2:
        widest = jnp.max(jnp.maximum(count, _swap(count, "pix")))
    else:
        widest = lax.pmax(jnp.max(count), "pix")

    order = jnp.cumsum(keep.astype(jnp.int32), axis=1) - 1
    picks = keep[:, :, None] & (order[:, :, None] == jnp.arange(slots, dtype=jnp.int32)[None, None, :])
    picks = picks.astype(jnp.bfloat16)

    def cut(frames):
        pieces = [
            jnp.dot(frames[:, i * chunk:(i + 1) * chunk], picks[i], preferred_element_type=jnp.float32)
            for i in range(n_chunk)
        ]
        return jnp.concatenate(pieces, axis=1).astype(frames.dtype)

    hi = lax.reduce_precision(factor, exponent_bits=8, mantissa_bits=7)
    mid = lax.reduce_precision(factor - hi, exponent_bits=8, mantissa_bits=7)
    lo = factor - hi - mid
    table = jnp.stack([hi, mid, lo, qbin.astype(jnp.float32)]).astype(jnp.bfloat16)
    table = jnp.concatenate(
        [jnp.dot(table[:, i * chunk:(i + 1) * chunk], picks[i], preferred_element_type=jnp.float32)
         for i in range(n_chunk)],
        axis=1,
    )
    table = jnp.stack([(table[0] + table[1]) + table[2], table[3]])
    used = (jnp.arange(slots, dtype=jnp.int32)[None, :] < count[:, None]).astype(jnp.float32)
    cut_operands = (cut(sample_frames).T, cut(reference_frames).T, table, used.reshape(-1))

    def compact(operands):
        cut_sample, cut_reference, table, used = operands[2]
        return pipeline(cut_sample, cut_reference, table[0], table[1].astype(jnp.int32), used, full)

    def whole(operands):
        sample_frames, reference_frames, _ = operands
        return pipeline(sample_frames.T, reference_frames.T, factor, qbin, sample_weight, full)

    out = lax.cond(widest <= slots, compact, whole, (sample_frames, reference_frames, cut_operands))
    return out[:, :, None, :]


def solution(mesh):
    return jax.shard_map(
        on_device,
        mesh=mesh,
        in_specs=(
            P(("row", "col"), "pix"),
            P(("row", "col"), "pix"),
            P("pix"),
            P("pix"),
            P("pix"),
            P("pix"),
            P("pix"),
        ),
        out_specs=P("row", None, "col", "pix"),
        check_vma=False,
    )
```
